128 devices in a mesh: expert: 4 (over z_lo, core), fsdp: 32 (over y, z_hi, x).
Axes of the slice: x: 4, y: 4, z: 4 (z_hi: 2, z_lo: 2; z = z_hi * 2 + z_lo), core: 2. Of those that a mesh axis runs over, the one named last changes fastest.
Arguments:
- tokens: bfloat16 [16384, 2048], P(('expert', 'fsdp')), may hold values from -6 to 6
- expert_ids: int32 [16384, 1], P(('expert', 'fsdp')), may hold values from 0 to 7; in each aligned block of 128 rows (0 to 127, 128 to 255, ...) at most 24 rows name the same one
- gate_weight: bfloat16 [8, 2048, 8192], P('expert', None, 'fsdp'), may hold values from -0.125 to 0.125
- up_weight: bfloat16 [8, 2048, 8192], P('expert', None, 'fsdp'), may hold values from -0.125 to 0.125
- hidden_grad: bfloat16 [8, 3072, 8192], P('expert', None, 'fsdp'), may hold values from -0.1796875 to 0.1796875
Outputs:
- hidden: bfloat16 [8, 3072, 8192], P('expert', None, 'fsdp')
- gate_grad: float32 [8, 2048, 8192], P('expert', None, 'fsdp')
- up_grad: float32 [8, 2048, 8192], P('expert', None, 'fsdp')
The draws below stay inside these ranges and needn't reach their ends.
Inputs may be any that keep to these rules, and one draw needn't show every extreme that they name: `expert_ids`: within the tokens of one device (aligned blocks of 128 rows) no expert is named more than 24 times, a bound that some block reaches.
All inputs are finite; a program needn't handle non-finite values.
Results may differ from the reference program's by a relative error of at most 0.003.
Values may be sent and summed in bfloat16 or wider, within the bound.
No kernel may reach another device: no remote copies, remote signals or barrier semaphores. Data moves between devices by JAX's collectives and lax.ppermute only.
A program may use at most 192 MiB of HBM per device.

```python
import math
import jax
import jax.numpy as jnp
import numpy as np
from jax import lax

D = 2048
FF = 8192
TOK_DEV = 128
EXPERTS = 8
CAP = 24
TOKENS = 16384
SLOTS = 3072
N_EXPERT = 4
N_FSDP = 32


def block_scale(stream_key, dims, shards, least, top_value):
    def one(position, blocks):
        draws = jax.random.uniform(jax.random.fold_in(jax.random.fold_in(stream_key, 6), position), (blocks,), jnp.float32, least / len(shards), top_value / len(shards))
        return jnp.repeat(jnp.exp(draws), dims[position] // blocks).reshape((-1,) + (1,) * (len(dims) - position - 1))

    level = one(*shards[0])
    for cut in shards[1:]:
        level = level * one(*cut)
    return level


def deal_out(own_key, own, number, rows, number_of, top, reach, skew):
    order = jax.random.permutation(own_key, number_of)
    packed, ordinary = shares(number_of, rows * top, reach, skew, True), shares(number_of, rows * top, reach, skew, False)
    places = jnp.arange(number_of)

    def named(tallies, rotation):
        used = int((tallies > 0).sum())
        fixed = max(1, used // 4)
        passed = fixed + (places - fixed + rotation * (used - fixed)) % max(1, number_of - fixed)
        return jnp.zeros((number_of,), jnp.int32).at[order[jnp.where(places < fixed, places, passed)]].set(jnp.asarray(tallies, jnp.int32))

    tallies = jnp.where(number % 4 == 0, named(packed, number // 4), named(ordinary, number - number // 4 - 1))
    mixed = jax.random.permutation(jax.random.fold_in(own, 3), number_of)
    donor, sink = mixed[0:number_of // 2 * 2:2], mixed[1:number_of // 2 * 2:2]
    room = jnp.minimum(tallies[donor] - 1, reach - tallies[sink]) // 2
    room = jnp.where((donor == order[0]) | (sink == order[0]) | (tallies[sink] == 0), 0, jnp.maximum(room, 0))
    passed = jax.random.randint(jax.random.fold_in(own, 4), (number_of // 2,), 0, 1 << 20) % (room + 1)
    tallies = tallies.at[donor].add(-passed).at[sink].add(passed)
    members = jnp.searchsorted(jnp.cumsum(tallies), jnp.arange(rows * top), side="right").astype(jnp.int32)
    grid = members.reshape(top, rows).T
    grid = grid[jax.random.permutation(jax.random.fold_in(own, 1), rows)]
    rotation = jax.random.randint(jax.random.fold_in(own, 2), (rows, 1), 0, top)
    return jnp.take_along_axis(grid, (jnp.arange(top)[None, :] + rotation) % top, axis=1)


def shares(count, total, bound, skew, full):
    loads = [(1 << 20) // math.isqrt(grade ** skew) + 1 for grade in range(1, count + 1)]
    largest = bound if full else min(bound, max(-(-total // count), total * loads[0] // sum(loads)))
    least = 1 if total - largest >= count - 1 else 0
    given, spare = [largest] + [least] * (count - 1), total - largest - least * (count - 1)
    while spare > 0:
        free = [i for i in range(1, count) if given[i] < largest] or [i for i in range(1, count) if given[i] < bound]
        whole, budget = sum([loads[i] for i in free]), spare
        for i in free:
            addition = min(bound - given[i], max(1, budget * loads[i] // whole), spare)
            given[i] = given[i] + addition
            spare = spare - addition
    return np.array(given)


def bell_draw(rng, dims, spread, bound, split=(), kind=jnp.bfloat16):
    gain = block_scale(rng, dims, split, -0.22, 0.18) if split else 1.0
    entries = jax.random.normal(rng, dims, jnp.float32) * spread * gain
    return jnp.minimum(jnp.maximum(entries, -bound), bound).astype(kind)


def setup_inputs(seed: int = 0) -> dict:
    seeds = jax.random.split(jax.random.key(seed), 6)
    tokens = bell_draw(seeds[0], (TOKENS, D), 1.0, 6.0, ((0, 128),))
    expert_ids_keys = jax.random.split(jax.random.fold_in(seeds[1], 1), TOKENS // TOK_DEV)
    expert_ids_turns = jax.random.permutation(jax.random.fold_in(seeds[1], 3), TOKENS // TOK_DEV)
    expert_ids = jax.vmap(lambda own, number: deal_out(jax.random.fold_in(seeds[1], 2), own, number, TOK_DEV, EXPERTS, 1, CAP, 2))(expert_ids_keys, expert_ids_turns).reshape((TOKENS, 1))
    gate_weight = bell_draw(seeds[2], (EXPERTS, D, FF), D ** -0.5, 0.125, ((0, 4), (2, 32)))
    up_weight = bell_draw(seeds[3], (EXPERTS, D, FF), D ** -0.5, 0.125, ((0, 4), (2, 32)))
    hidden_grad = bell_draw(seeds[4], (EXPERTS, SLOTS, FF), 0.03, 0.1796875, ((0, 4), (2, 32)))
    return {"tokens": tokens, "expert_ids": expert_ids, "gate_weight": gate_weight, "up_weight": up_weight, "hidden_grad": hidden_grad}


def expert_pass(args):
    rows, gate_w, up_w, cotan = args
    gate = jnp.dot(rows, gate_w, preferred_element_type=jnp.float32)
    upval = jnp.dot(rows, up_w, preferred_element_type=jnp.float32)
    sigma = 1.0 / (1.0 + jnp.exp(-gate))
    active = gate * sigma
    hidden = (active * upval).astype(jnp.bfloat16)
    cot = cotan.astype(jnp.float32)
    gate_delta = (cot * upval * sigma * (1.0 + gate * (1.0 - sigma))).astype(jnp.bfloat16)
    up_delta = (cot * active).astype(jnp.bfloat16)
    gate_grad = jnp.dot(rows.T, gate_delta, preferred_element_type=jnp.float32)
    up_grad = jnp.dot(rows.T, up_delta, preferred_element_type=jnp.float32)
    return hidden, gate_grad, up_grad


def reference(tokens, expert_ids, gate_weight, up_weight, hidden_grad):
    route = expert_ids[:, 0].astype(jnp.int32)
    blocks = N_EXPERT * N_FSDP
    grouped = route.reshape(blocks, TOK_DEV)
    onehot = (grouped[:, :, None] == jnp.arange(EXPERTS, dtype=jnp.int32)[None, None, :]).astype(jnp.int32)
    before = jnp.cumsum(onehot, axis=1) - onehot
    rank = jnp.sum(before * onehot, axis=2).astype(jnp.int32)
    slot = (jnp.arange(blocks, dtype=jnp.int32)[:, None] * CAP + rank).reshape(-1).astype(jnp.int32)
    dispatched = jnp.zeros((EXPERTS, SLOTS, D), jnp.bfloat16).at[route, slot].set(tokens)
    hidden, gate_grad, up_grad = lax.map(expert_pass, (dispatched, gate_weight, up_weight, hidden_grad))
    return hidden, gate_grad, up_grad
```

```python
import jax
import jax.numpy as jnp
from jax import lax
from jax.sharding import PartitionSpec as P

CAP = 24


def chunk_pass(rows, gate_w, up_w, cotan):
    gate = jnp.einsum("grd,gdf->grf", rows, gate_w, preferred_element_type=jnp.float32)
    upval = jnp.einsum("grd,gdf->grf", rows, up_w, preferred_element_type=jnp.float32)
    cotan = cotan.astype(jnp.float32)
    sigma = 1.0 / (1.0 + jnp.exp(-gate))
    active = gate * sigma
    hidden = (active * upval).astype(jnp.bfloat16)
    gate_delta = (cotan * upval * sigma * (1.0 + gate * (1.0 - sigma))).astype(jnp.bfloat16)
    up_delta = (cotan * active).astype(jnp.bfloat16)
    gate_sum = jnp.einsum("grd,grf->gdf", rows, gate_delta, preferred_element_type=jnp.float32)
    up_sum = jnp.einsum("grd,grf->gdf", rows, up_delta, preferred_element_type=jnp.float32)
    return hidden, gate_sum, up_sum


def on_device(tokens, expert_ids, gate_weight, up_weight, hidden_grad):
    owners = lax.axis_size("expert")
    members = lax.axis_size("fsdp")
    per_owner = gate_weight.shape[0]
    model = gate_weight.shape[1]
    route = expert_ids[:, 0]
    total_experts = per_owner * owners
    onehot = (route[:, None] == jnp.arange(total_experts, dtype=jnp.int32)[None, :]).astype(
        jnp.int32
    )
    rank = jnp.sum((jnp.cumsum(onehot, axis=0) - onehot) * onehot, axis=1)
    owner_of = route // per_owner
    within = route % per_owner
    target = owner_of * (per_owner * CAP) + within * CAP + rank
    send_rows = per_owner * owners * CAP
    placing = (jnp.arange(send_rows, dtype=jnp.int32)[:, None] == target[None, :]).astype(
        jnp.bfloat16
    )
    outgoing = jnp.dot(placing, tokens, preferred_element_type=jnp.float32).astype(jnp.bfloat16)
    outgoing = outgoing.reshape(owners, per_owner, CAP, model)
    arrived = lax.all_to_all(outgoing, "expert", split_axis=0, concat_axis=0, tiled=True)
    slot_count = members * CAP

    def gather(source):
        piece = lax.dynamic_index_in_dim(arrived, source, axis=0, keepdims=False)
        return lax.all_gather(piece, "fsdp", axis=1, tiled=True)

    def step(source, rows, hidden_buf, gate_acc, up_acc):
        start = source * slot_count
        cotan = lax.dynamic_slice_in_dim(hidden_grad, start, slot_count, axis=1)
        hidden, gate_sum, up_sum = chunk_pass(rows, gate_weight, up_weight, cotan)
        hidden_buf = lax.dynamic_update_slice_in_dim(hidden_buf, hidden, start, axis=1)
        return hidden_buf, gate_acc + gate_sum, up_acc + up_sum

    def body(source, carry):
        rows, hidden_buf, gate_acc, up_acc = carry
        next_rows = gather(source + 1)
        hidden_buf, gate_acc, up_acc = step(source, rows, hidden_buf, gate_acc, up_acc)
        return next_rows, hidden_buf, gate_acc, up_acc

    hidden_buf = jnp.zeros(hidden_grad.shape, jnp.bfloat16)
    gate_acc = jnp.zeros(gate_weight.shape, jnp.float32)
    up_acc = jnp.zeros(up_weight.shape, jnp.float32)
    rows = gather(0)
    rows, hidden_buf, gate_acc, up_acc = lax.fori_loop(
        0, owners - 1, body, (rows, hidden_buf, gate_acc, up_acc)
    )
    hidden_buf, gate_acc, up_acc = step(owners - 1, rows, hidden_buf, gate_acc, up_acc)
    return (hidden_buf, gate_acc, up_acc)


def solution(mesh):
    in_specs = (
        P(("expert", "fsdp"), None),
        P(("expert", "fsdp"), None),
        P("expert", None, "fsdp"),
        P("expert", None, "fsdp"),
        P("expert", None, "fsdp"),
    )
    out_specs = (P("expert", None, "fsdp"), P("expert", None, "fsdp"), P("expert", None, "fsdp"))
    return jax.shard_map(
        on_device, mesh=mesh, in_specs=in_specs, out_specs=out_specs, check_vma=False
    )
```

```python
import jax
import jax.numpy as jnp
from jax import lax
from jax.sharding import Mesh
from jax.sharding import PartitionSpec as P

CAP = 24
FSDP_AXES = ("y", "zh", "x")


def shift(value, axis, step):
    size = lax.axis_size(axis)
    return lax.ppermute(value, axis, [(j, (j + step) % size) for j in range(size)])


def ring_gather(value, axis, split_axis):
    from_minus = shift(value, axis, 1)
    from_plus = shift(value, axis, -1)
    half = value.shape[split_axis] // 2
    first = lax.slice_in_dim(from_minus, 0, half, axis=split_axis)
    second = lax.slice_in_dim(from_plus, half, value.shape[split_axis], axis=split_axis)
    far = jnp.concatenate([shift(first, axis, 1), shift(second, axis, -1)], axis=split_axis)
    return jnp.stack([value, from_plus, far, from_minus], axis=1)


def chunk_pass(rows, gate_w, up_w, cotan):
    gate = jnp.einsum("grd,gdf->grf", rows, gate_w, preferred_element_type=jnp.float32)
    upval = jnp.einsum("grd,gdf->grf", rows, up_w, preferred_element_type=jnp.float32)
    cotan = cotan.astype(jnp.float32)
    sigma = 1.0 / (1.0 + jnp.exp(-gate))
    active = gate * sigma
    hidden = (active * upval).astype(jnp.bfloat16)
    gate_delta = (cotan * upval * sigma * (1.0 + gate * (1.0 - sigma))).astype(jnp.bfloat16)
    up_delta = (cotan * active).astype(jnp.bfloat16)
    gate_sum = jnp.einsum("grd,grf->gdf", rows, gate_delta, preferred_element_type=jnp.float32)
    up_sum = jnp.einsum("grd,grf->gdf", rows, up_delta, preferred_element_type=jnp.float32)
    return hidden, gate_sum, up_sum


def on_device(tokens, expert_ids, gate_weight, up_weight, hidden_grad):
    owners = lax.axis_size("expert")
    per_owner = gate_weight.shape[0]
    model = gate_weight.shape[1]
    width = gate_weight.shape[2]
    route = expert_ids[:, 0]
    total_experts = per_owner * owners
    onehot = (route[:, None] == jnp.arange(total_experts, dtype=jnp.int32)[None, :]).astype(
        jnp.int32
    )
    rank = jnp.sum((jnp.cumsum(onehot, axis=0) - onehot) * onehot, axis=1)
    owner_of = route // per_owner
    within = route % per_owner
    target = within * (owners * CAP) + owner_of * CAP + rank
    send_rows = per_owner * owners * CAP
    placing = (jnp.arange(send_rows, dtype=jnp.int32)[:, None] == target[None, :]).astype(
        jnp.bfloat16
    )
    outgoing = jnp.dot(placing, tokens, preferred_element_type=jnp.float32).astype(jnp.bfloat16)
    outgoing = outgoing.reshape(per_owner, owners, CAP, model)
    arrived = lax.all_to_all(outgoing, "expert", split_axis=1, concat_axis=1, tiled=True)

    ny, nz, nx = (lax.axis_size(a) for a in FSDP_AXES)
    py, pz, px = (lax.axis_index(a) for a in FSDP_AXES)
    local = jnp.stack([arrived, shift(arrived, "zh", 1)], axis=1)
    split = owners // 2
    half_a = local[:, :, :split]
    half_b = local[:, :, split:]
    rows_a = ring_gather(ring_gather(half_a, "x", 4), "y", 5)
    rows_b = ring_gather(ring_gather(half_b, "y", 4), "x", 5)

    grad = hidden_grad.reshape(per_owner, owners, ny, nz, nx, CAP, width)
    grad = jnp.roll(grad, -py, axis=2)
    grad = jnp.roll(grad, -pz, axis=3)
    grad = jnp.roll(grad, -px, axis=4)
    grad_a = jnp.transpose(grad[:, :split], (0, 2, 4, 3, 1, 5, 6))
    grad_b = jnp.transpose(grad[:, split:], (0, 4, 2, 3, 1, 5, 6))

    count = split * ny * nz * nx * CAP
    hid_a, gate_a, up_a = chunk_pass(
        rows_a.reshape(per_owner, count, model), gate_weight, up_weight,
        grad_a.reshape(per_owner, count, width),
    )
    hid_b, gate_b, up_b = chunk_pass(
        rows_b.reshape(per_owner, count, model), gate_weight, up_weight,
        grad_b.reshape(per_owner, count, width),
    )
    hid_a = jnp.transpose(hid_a.reshape(per_owner, ny, nx, nz, split, CAP, width), (0, 4, 1, 3, 2, 5, 6))
    hid_b = jnp.transpose(hid_b.reshape(per_owner, nx, ny, nz, split, CAP, width), (0, 4, 2, 3, 1, 5, 6))
    hidden = jnp.concatenate([hid_a, hid_b], axis=1)
    hidden = jnp.roll(hidden, py, axis=2)
    hidden = jnp.roll(hidden, pz, axis=3)
    hidden = jnp.roll(hidden, px, axis=4)
    hidden = hidden.reshape(hidden_grad.shape)
    return (hidden, gate_a + gate_b, up_a + up_b)


def solution(mesh):
    grid = Mesh(mesh.devices.reshape(mesh.shape["expert"], 4, 2, -1), ("expert",) + FSDP_AXES)
    rows_spec = P(("expert",) + FSDP_AXES, None)
    expert_spec = P("expert", None, FSDP_AXES)
    in_specs = (rows_spec, rows_spec, expert_spec, expert_spec, expert_spec)
    out_specs = (expert_spec, expert_spec, expert_spec)
    return jax.shard_map(
        on_device, mesh=grid, in_specs=in_specs, out_specs=out_specs, check_vma=False
    )
```

```python
import jax
import jax.numpy as jnp
from jax import lax
from jax.sharding import Mesh
from jax.sharding import PartitionSpec as P

CAP = 24
FSDP_AXES = ("y", "zh", "x")


def shift(value, axis, step):
    size = lax.axis_size(axis)
    return lax.ppermute(value, axis, [(j, (j + step) % size) for j in range(size)])


def paired_ring(first, first_axis, second, second_axis, split_axis):
    first_minus = shift(first, first_axis, 1)
    first_plus = shift(first, first_axis, -1)
    second_minus = shift(second, second_axis, 1)
    second_plus = shift(second, second_axis, -1)
    first_minus, first_plus, second_minus, second_plus = lax.optimization_barrier(
        (first_minus, first_plus, second_minus, second_plus)
    )
    half = first.shape[split_axis] // 2
    size = first.shape[split_axis]

    def far(minus, plus, axis):
        lo = shift(lax.slice_in_dim(minus, 0, half, axis=split_axis), axis, 1)
        hi = shift(lax.slice_in_dim(plus, half, size, axis=split_axis), axis, -1)
        return lo, hi

    first_lo, first_hi = far(first_minus, first_plus, first_axis)
    second_lo, second_hi = far(second_minus, second_plus, second_axis)
    first_lo, first_hi, second_lo, second_hi = lax.optimization_barrier(
        (first_lo, first_hi, second_lo, second_hi)
    )
    first_far = jnp.concatenate([first_lo, first_hi], axis=split_axis)
    second_far = jnp.concatenate([second_lo, second_hi], axis=split_axis)
    first_all = jnp.stack([first, first_plus, first_far, first_minus], axis=1)
    second_all = jnp.stack([second, second_plus, second_far, second_minus], axis=1)
    return first_all, second_all


def chunk_pass(rows, gate_w, up_w, cotan):
    gate = jnp.einsum("grd,gdf->grf", rows, gate_w, preferred_element_type=jnp.float32)
    upval = jnp.einsum("grd,gdf->grf", rows, up_w, preferred_element_type=jnp.float32)
    cotan = cotan.astype(jnp.float32)
    sigma = 1.0 / (1.0 + jnp.exp(-gate))
    active = gate * sigma
    hidden = (active * upval).astype(jnp.bfloat16)
    gate_delta = (cotan * upval * sigma * (1.0 + gate * (1.0 - sigma))).astype(jnp.bfloat16)
    up_delta = (cotan * active).astype(jnp.bfloat16)
    gate_sum = jnp.einsum("grd,grf->gdf", rows, gate_delta, preferred_element_type=jnp.float32)
    up_sum = jnp.einsum("grd,grf->gdf", rows, up_delta, preferred_element_type=jnp.float32)
    return hidden, gate_sum, up_sum


def on_device(tokens, expert_ids, gate_weight, up_weight, hidden_grad):
    owners = lax.axis_size("expert")
    per_owner = gate_weight.shape[0]
    model = gate_weight.shape[1]
    width = gate_weight.shape[2]
    route = expert_ids[:, 0]
    total_experts = per_owner * owners
    onehot = (route[:, None] == jnp.arange(total_experts, dtype=jnp.int32)[None, :]).astype(
        jnp.int32
    )
    rank = jnp.sum((jnp.cumsum(onehot, axis=0) - onehot) * onehot, axis=1)
    owner_of = route // per_owner
    within = route % per_owner
    target = within * (owners * CAP) + owner_of * CAP + rank
    send_rows = per_owner * owners * CAP
    placing = (jnp.arange(send_rows, dtype=jnp.int32)[:, None] == target[None, :]).astype(
        jnp.bfloat16
    )
    outgoing = jnp.dot(placing, tokens, preferred_element_type=jnp.float32).astype(jnp.bfloat16)
    outgoing = outgoing.reshape(per_owner, owners, CAP, model)
    arrived = lax.all_to_all(outgoing, "expert", split_axis=1, concat_axis=1, tiled=True)

    ny, nz, nx = (lax.axis_size(a) for a in FSDP_AXES)
    py, pz, px = (lax.axis_index(a) for a in FSDP_AXES)
    local = jnp.stack([arrived, shift(arrived, "zh", 1)], axis=1)
    split = owners // 2
    half_a = local[:, :, :split]
    half_b = local[:, :, split:]
    stage_a, stage_b = paired_ring(half_a, "x", half_b, "y", 4)
    rows_a, rows_b = paired_ring(stage_a, "y", stage_b, "x", 5)

    grad = hidden_grad.reshape(per_owner, owners, ny, nz, nx, CAP, width)
    grad = jnp.roll(grad, -py, axis=2)
    grad = jnp.roll(grad, -pz, axis=3)
    grad = jnp.roll(grad, -px, axis=4)
    grad_a = jnp.transpose(grad[:, :split], (0, 2, 4, 3, 1, 5, 6))
    grad_b = jnp.transpose(grad[:, split:], (0, 4, 2, 3, 1, 5, 6))

    count = split * ny * nz * nx * CAP
    hid_a, gate_a, up_a = chunk_pass(
        rows_a.reshape(per_owner, count, model), gate_weight, up_weight,
        grad_a.reshape(per_owner, count, width),
    )
    hid_b, gate_b, up_b = chunk_pass(
        rows_b.reshape(per_owner, count, model), gate_weight, up_weight,
        grad_b.reshape(per_owner, count, width),
    )
    hid_a = jnp.transpose(hid_a.reshape(per_owner, ny, nx, nz, split, CAP, width), (0, 4, 1, 3, 2, 5, 6))
    hid_b = jnp.transpose(hid_b.reshape(per_owner, nx, ny, nz, split, CAP, width), (0, 4, 2, 3, 1, 5, 6))
    hidden = jnp.concatenate([hid_a, hid_b], axis=1)
    hidden = jnp.roll(hidden, py, axis=2)
    hidden = jnp.roll(hidden, pz, axis=3)
    hidden = jnp.roll(hidden, px, axis=4)
    hidden = hidden.reshape(hidden_grad.shape)
    return (hidden, gate_a + gate_b, up_a + up_b)


def solution(mesh):
    grid = Mesh(mesh.devices.reshape(mesh.shape["expert"], 4, 2, -1), ("expert",) + FSDP_AXES)
    rows_spec = P(("expert",) + FSDP_AXES, None)
    expert_spec = P("expert", None, FSDP_AXES)
    in_specs = (rows_spec, rows_spec, expert_spec, expert_spec, expert_spec)
    out_specs = (expert_spec, expert_spec, expert_spec)
    return jax.shard_map(
        on_device, mesh=grid, in_specs=in_specs, out_specs=out_specs, check_vma=False
    )
```

```python
import jax
import jax.numpy as jnp
from jax import lax
from jax.sharding import Mesh
from jax.sharding import PartitionSpec as P

CAP = 24
FSDP_AXES = ("y", "zh", "x")


def shift(value, axis, step):
    size = lax.axis_size(axis)
    return lax.ppermute(value, axis, [(j, (j + step) % size) for j in range(size)])


def paired_ring(first, first_axis, second, second_axis):
    first_minus = shift(first, first_axis, 1)
    first_plus = shift(first, first_axis, -1)
    second_minus = shift(second, second_axis, 1)
    second_plus = shift(second, second_axis, -1)
    first_minus, first_plus, second_minus, second_plus = lax.optimization_barrier(
        (first_minus, first_plus, second_minus, second_plus)
    )
    half = first.shape[0] // 2

    def far(minus, plus, axis):
        return shift(minus[:half], axis, 1), shift(plus[half:], axis, -1)

    first_lo, first_hi = far(first_minus, first_plus, first_axis)
    second_lo, second_hi = far(second_minus, second_plus, second_axis)
    first_lo, first_hi, second_lo, second_hi = lax.optimization_barrier(
        (first_lo, first_hi, second_lo, second_hi)
    )
    first_far = jnp.concatenate([first_lo, first_hi], axis=0)
    second_far = jnp.concatenate([second_lo, second_hi], axis=0)
    return [first, first_plus, first_far, first_minus], [second, second_plus, second_far, second_minus]


def chunk_pass(rows, gate_w, up_w, cotan):
    gate = jnp.dot(rows, gate_w, preferred_element_type=jnp.float32)
    upval = jnp.dot(rows, up_w, preferred_element_type=jnp.float32)
    cotan = cotan.astype(jnp.float32)
    sigma = 1.0 / (1.0 + jnp.exp(-gate))
    active = gate * sigma
    hidden = (active * upval).astype(jnp.bfloat16)
    gate_delta = (cotan * upval * sigma * (1.0 + gate * (1.0 - sigma))).astype(jnp.bfloat16)
    up_delta = (cotan * active).astype(jnp.bfloat16)
    gate_sum = jnp.dot(rows.T, gate_delta, preferred_element_type=jnp.float32)
    up_sum = jnp.dot(rows.T, up_delta, preferred_element_type=jnp.float32)
    return hidden, gate_sum, up_sum


def on_device(tokens, expert_ids, gate_weight, up_weight, hidden_grad):
    owners = lax.axis_size("expert")
    per_owner = gate_weight.shape[0]
    model = gate_weight.shape[1]
    width = gate_weight.shape[2]
    route = expert_ids[:, 0]
    total_experts = per_owner * owners
    onehot = (route[:, None] == jnp.arange(total_experts, dtype=jnp.int32)[None, :]).astype(
        jnp.int32
    )
    rank = jnp.sum((jnp.cumsum(onehot, axis=0) - onehot) * onehot, axis=1)
    owner_of = route // per_owner
    within = route % per_owner
    target = owner_of * (per_owner * CAP) + within * CAP + rank
    send_rows = per_owner * owners * CAP
    placing = (jnp.arange(send_rows, dtype=jnp.int32)[:, None] == target[None, :]).astype(
        jnp.bfloat16
    )
    outgoing = jnp.dot(placing, tokens, preferred_element_type=jnp.float32).astype(jnp.bfloat16)
    outgoing = outgoing.reshape(owners, per_owner, CAP, model)
    arrived = lax.all_to_all(outgoing, "expert", split_axis=0, concat_axis=0, tiled=True)
    by_expert = jnp.transpose(arrived, (1, 0, 2, 3)).reshape(per_owner, owners * CAP, model)

    ny, nz, nx = (lax.axis_size(a) for a in FSDP_AXES)
    py, pz, px = (lax.axis_index(a) for a in FSDP_AXES)
    local = jnp.stack([by_expert, shift(by_expert, "zh", 1)], axis=1)
    local = local.reshape(per_owner, nz * owners * CAP, model)
    stage_a, stage_b = paired_ring(local[0], "x", local[1], "y")
    stage_a = jnp.concatenate(stage_a, axis=0)
    stage_b = jnp.concatenate(stage_b, axis=0)
    final_a, final_b = paired_ring(stage_a, "y", stage_b, "x")
    rest_a = jnp.concatenate(final_a[1:], axis=0)
    rest_b = jnp.concatenate(final_b[1:], axis=0)

    grad = hidden_grad.reshape(per_owner, owners, ny, nz, nx, CAP, width)
    grad = jnp.roll(grad, -py, axis=2)
    grad = jnp.roll(grad, -pz, axis=3)
    grad = jnp.roll(grad, -px, axis=4)
    block = nx * nz * owners * CAP
    grad_a = jnp.transpose(grad[0], (1, 3, 2, 0, 4, 5)).reshape(ny, block, width)
    grad_b = jnp.transpose(grad[1], (3, 1, 2, 0, 4, 5)).reshape(nx, block, width)

    h_a0, g_a0, u_a0 = chunk_pass(stage_a, gate_weight[0], up_weight[0], grad_a[0])
    h_b0, g_b0, u_b0 = chunk_pass(stage_b, gate_weight[1], up_weight[1], grad_b[0])
    h_a1, g_a1, u_a1 = chunk_pass(
        rest_a, gate_weight[0], up_weight[0], grad_a[1:].reshape(-1, width)
    )
    h_b1, g_b1, u_b1 = chunk_pass(
        rest_b, gate_weight[1], up_weight[1], grad_b[1:].reshape(-1, width)
    )
    hid_a = jnp.concatenate([h_a0, h_a1], axis=0).reshape(ny, nx, nz, owners, CAP, width)
    hid_b = jnp.concatenate([h_b0, h_b1], axis=0).reshape(nx, ny, nz, owners, CAP, width)
    hidden = jnp.stack(
        [jnp.transpose(hid_a, (3, 0, 2, 1, 4, 5)), jnp.transpose(hid_b, (3, 1, 2, 0, 4, 5))], axis=0
    )
    hidden = jnp.roll(hidden, py, axis=2)
    hidden = jnp.roll(hidden, pz, axis=3)
    hidden = jnp.roll(hidden, px, axis=4)
    hidden = hidden.reshape(hidden_grad.shape)
    gate_grad = jnp.stack([g_a0 + g_a1, g_b0 + g_b1], axis=0)
    up_grad = jnp.stack([u_a0 + u_a1, u_b0 + u_b1], axis=0)
    return (hidden, gate_grad, up_grad)


def solution(mesh):
    grid = Mesh(mesh.devices.reshape(mesh.shape["expert"], 4, 2, -1), ("expert",) + FSDP_AXES)
    rows_spec = P(("expert",) + FSDP_AXES, None)
    expert_spec = P("expert", None, FSDP_AXES)
    in_specs = (rows_spec, rows_spec, expert_spec, expert_spec, expert_spec)
    out_specs = (expert_spec, expert_spec, expert_spec)
    return jax.shard_map(
        on_device, mesh=grid, in_specs=in_specs, out_specs=out_specs, check_vma=False
    )
```

```python
import jax
import jax.numpy as jnp
from jax import lax
from jax.sharding import Mesh
from jax.sharding import PartitionSpec as P

CAP = 24
FSDP_AXES = ("y", "zh", "x")


def shift(value, axis, step):
    size = lax.axis_size(axis)
    return lax.ppermute(value, axis, [(j, (j + step) % size) for j in range(size)])


def paired_ring(first, first_axis, second, second_axis):
    first_minus = shift(first, first_axis, 1)
    first_plus = shift(first, first_axis, -1)
    second_minus = shift(second, second_axis, 1)
    second_plus = shift(second, second_axis, -1)
    first_minus, first_plus, second_minus, second_plus = lax.optimization_barrier(
        (first_minus, first_plus, second_minus, second_plus)
    )
    half = first.shape[0] // 2

    def far(minus, plus, axis):
        return shift(minus[:half], axis, 1), shift(plus[half:], axis, -1)

    first_lo, first_hi = far(first_minus, first_plus, first_axis)
    second_lo, second_hi = far(second_minus, second_plus, second_axis)
    first_lo, first_hi, second_lo, second_hi = lax.optimization_barrier(
        (first_lo, first_hi, second_lo, second_hi)
    )
    first_far = jnp.concatenate([first_lo, first_hi], axis=0)
    second_far = jnp.concatenate([second_lo, second_hi], axis=0)
    return [first, first_plus, first_far, first_minus], [second, second_plus, second_far, second_minus]


def chunk_pass(rows, gate_w, up_w, cotan):
    gate = jnp.dot(rows, gate_w, preferred_element_type=jnp.float32)
    upval = jnp.dot(rows, up_w, preferred_element_type=jnp.float32)
    cotan = cotan.astype(jnp.float32)
    sigma = 1.0 / (1.0 + jnp.exp(-gate))
    active = gate * sigma
    hidden = (active * upval).astype(jnp.bfloat16)
    gate_delta = (cotan * upval * sigma * (1.0 + gate * (1.0 - sigma))).astype(jnp.bfloat16)
    up_delta = (cotan * active).astype(jnp.bfloat16)
    gate_sum = jnp.dot(rows.T, gate_delta, preferred_element_type=jnp.float32)
    up_sum = jnp.dot(rows.T, up_delta, preferred_element_type=jnp.float32)
    return hidden, gate_sum, up_sum


def on_device(tokens, expert_ids, gate_weight, up_weight, hidden_grad):
    owners = lax.axis_size("expert")
    per_owner = gate_weight.shape[0]
    model = gate_weight.shape[1]
    width = gate_weight.shape[2]
    route = expert_ids[:, 0]
    total_experts = per_owner * owners
    onehot = (route[:, None] == jnp.arange(total_experts, dtype=jnp.int32)[None, :]).astype(
        jnp.int32
    )
    rank = jnp.sum((jnp.cumsum(onehot, axis=0) - onehot) * onehot, axis=1)
    owner_of = route // per_owner
    within = route % per_owner
    target = owner_of * (per_owner * CAP) + within * CAP + rank
    send_rows = per_owner * owners * CAP
    placing = (jnp.arange(send_rows, dtype=jnp.int32)[:, None] == target[None, :]).astype(
        jnp.bfloat16
    )
    outgoing = jnp.dot(placing, tokens, preferred_element_type=jnp.float32).astype(jnp.bfloat16)
    outgoing = outgoing.reshape(owners, per_owner, CAP, model)
    arrived = lax.all_to_all(outgoing, "expert", split_axis=0, concat_axis=0, tiled=True)
    by_expert = jnp.transpose(arrived, (1, 0, 2, 3)).reshape(per_owner, owners * CAP, model)

    ny, nz, nx = (lax.axis_size(a) for a in FSDP_AXES)
    py, pz, px = (lax.axis_index(a) for a in FSDP_AXES)
    local = jnp.stack([by_expert, shift(by_expert, "zh", 1)], axis=1)
    local = local.reshape(per_owner, nz * owners * CAP, model)
    stage_a, stage_b = paired_ring(local[0], "x", local[1], "y")
    stage_a = jnp.concatenate(stage_a, axis=0)
    stage_b = jnp.concatenate(stage_b, axis=0)
    final_a, final_b = paired_ring(stage_a, "y", stage_b, "x")
    near_a = jnp.concatenate([final_a[1], final_a[3]], axis=0)
    near_b = jnp.concatenate([final_b[1], final_b[3]], axis=0)

    grad = hidden_grad.reshape(per_owner, owners, ny, nz, nx, CAP, width)
    grad = jnp.roll(grad, -py, axis=2)
    grad = jnp.roll(grad, -pz, axis=3)
    grad = jnp.roll(grad, -px, axis=4)
    block = nx * nz * owners * CAP
    grad_a = jnp.transpose(grad[0], (1, 3, 2, 0, 4, 5)).reshape(ny, block, width)
    grad_b = jnp.transpose(grad[1], (3, 1, 2, 0, 4, 5)).reshape(nx, block, width)

    parts_a = []
    parts_b = []
    for rows_a, rows_b, pick in (
        (stage_a, stage_b, [0]),
        (near_a, near_b, [1, 3]),
        (final_a[2], final_b[2], [2]),
    ):
        cot_a = jnp.concatenate([grad_a[k] for k in pick], axis=0)
        cot_b = jnp.concatenate([grad_b[k] for k in pick], axis=0)
        parts_a.append(chunk_pass(rows_a, gate_weight[0], up_weight[0], cot_a))
        parts_b.append(chunk_pass(rows_b, gate_weight[1], up_weight[1], cot_b))

    def assemble(parts, lead, nxt):
        own, near, far = (p[0] for p in parts)
        plus, minus = near[:block], near[block:]
        rows = jnp.concatenate([own, plus, far, minus], axis=0)
        grads = [sum(p[i] for p in parts) for i in (1, 2)]
        return rows.reshape(lead, nxt, nz, owners, CAP, width), grads

    hid_a, (g_a, u_a) = assemble(parts_a, ny, nx)
    hid_b, (g_b, u_b) = assemble(parts_b, nx, ny)
    hidden = jnp.stack(
        [jnp.transpose(hid_a, (3, 0, 2, 1, 4, 5)), jnp.transpose(hid_b, (3, 1, 2, 0, 4, 5))], axis=0
    )
    hidden = jnp.roll(hidden, py, axis=2)
    hidden = jnp.roll(hidden, pz, axis=3)
    hidden = jnp.roll(hidden, px, axis=4)
    hidden = hidden.reshape(hidden_grad.shape)
    gate_grad = jnp.stack([g_a, g_b], axis=0)
    up_grad = jnp.stack([u_a, u_b], axis=0)
    return (hidden, gate_grad, up_grad)


def solution(mesh):
    grid = Mesh(mesh.devices.reshape(mesh.shape["expert"], 4, 2, -1), ("expert",) + FSDP_AXES)
    rows_spec = P(("expert",) + FSDP_AXES, None)
    expert_spec = P("expert", None, FSDP_AXES)
    in_specs = (rows_spec, rows_spec, expert_spec, expert_spec, expert_spec)
    out_specs = (expert_spec, expert_spec, expert_spec)
    return jax.shard_map(
        on_device, mesh=grid, in_specs=in_specs, out_specs=out_specs, check_vma=False
    )
```

```python
import jax
import jax.numpy as jnp
from jax import lax
from jax.sharding import Mesh
from jax.sharding import PartitionSpec as P

CAP = 24
FSDP_AXES = ("y", "zh", "x")


def shift(value, axis, step):
    size = lax.axis_size(axis)
    return lax.ppermute(value, axis, [(j, (j + step) % size) for j in range(size)])


def paired_ring(first, first_axis, second, second_axis):
    first_minus = shift(first, first_axis, 1)
    first_plus = shift(first, first_axis, -1)
    second_minus = shift(second, second_axis, 1)
    second_plus = shift(second, second_axis, -1)
    first_minus, first_plus, second_minus, second_plus = lax.optimization_barrier(
        (first_minus, first_plus, second_minus, second_plus)
    )
    half = first.shape[0] // 2

    def far(minus, plus, axis):
        return shift(minus[:half], axis, 1), shift(plus[half:], axis, -1)

    first_lo, first_hi = far(first_minus, first_plus, first_axis)
    second_lo, second_hi = far(second_minus, second_plus, second_axis)
    first_lo, first_hi, second_lo, second_hi = lax.optimization_barrier(
        (first_lo, first_hi, second_lo, second_hi)
    )
    first_far = jnp.concatenate([first_lo, first_hi], axis=0)
    second_far = jnp.concatenate([second_lo, second_hi], axis=0)
    return [first, first_plus, first_far, first_minus], [second, second_plus, second_far, second_minus]


def chunk_pass(rows, gate_w, up_w, cotan):
    gate = jnp.dot(rows, gate_w, preferred_element_type=jnp.float32)
    upval = jnp.dot(rows, up_w, preferred_element_type=jnp.float32)
    cotan = cotan.astype(jnp.float32)
    sigma = 1.0 / (1.0 + jnp.exp(-gate))
    active = gate * sigma
    hidden = (active * upval).astype(jnp.bfloat16)
    gate_delta = (cotan * upval * sigma * (1.0 + gate * (1.0 - sigma))).astype(jnp.bfloat16)
    up_delta = (cotan * active).astype(jnp.bfloat16)
    gate_sum = jnp.dot(rows.T, gate_delta, preferred_element_type=jnp.float32)
    up_sum = jnp.dot(rows.T, up_delta, preferred_element_type=jnp.float32)
    return hidden, gate_sum, up_sum


def on_device(tokens, expert_ids, gate_weight, up_weight, hidden_grad):
    owners = lax.axis_size("expert")
    per_owner = gate_weight.shape[0]
    model = gate_weight.shape[1]
    width = gate_weight.shape[2]
    route = expert_ids[:, 0]
    total_experts = per_owner * owners
    onehot = (route[:, None] == jnp.arange(total_experts, dtype=jnp.int32)[None, :]).astype(
        jnp.int32
    )
    rank = jnp.sum((jnp.cumsum(onehot, axis=0) - onehot) * onehot, axis=1)
    owner_of = route // per_owner
    within = route % per_owner
    target = owner_of * (per_owner * CAP) + within * CAP + rank
    send_rows = per_owner * owners * CAP
    placing = (jnp.arange(send_rows, dtype=jnp.int32)[:, None] == target[None, :]).astype(
        jnp.bfloat16
    )
    outgoing = jnp.dot(placing, tokens, preferred_element_type=jnp.float32).astype(jnp.bfloat16)
    outgoing = outgoing.reshape(owners, per_owner, CAP, model)
    arrived = lax.all_to_all(outgoing, "expert", split_axis=0, concat_axis=0, tiled=True)
    by_expert = jnp.transpose(arrived, (1, 0, 2, 3)).reshape(per_owner, owners * CAP, model)

    ny, nz, nx = (lax.axis_size(a) for a in FSDP_AXES)
    py, pz, px = (lax.axis_index(a) for a in FSDP_AXES)
    local = jnp.stack([by_expert, shift(by_expert, "zh", 1)], axis=1)
    local = local.reshape(per_owner, nz * owners * CAP, model)
    stage_a, stage_b = paired_ring(local[0], "x", local[1], "y")
    stage_a = jnp.concatenate(stage_a, axis=0)
    stage_b = jnp.concatenate(stage_b, axis=0)
    final_a, final_b = paired_ring(stage_a, "y", stage_b, "x")
    near_a = jnp.concatenate([final_a[1], final_a[3]], axis=0)
    near_b = jnp.concatenate([final_b[1], final_b[3]], axis=0)

    grad = hidden_grad.reshape(per_owner, owners, ny, nz, nx, CAP, width)
    grad = jnp.roll(grad, -py, axis=2)
    grad = jnp.roll(grad, -pz, axis=3)
    grad = jnp.roll(grad, -px, axis=4)
    block = nx * nz * owners * CAP
    grad_a = jnp.transpose(grad[0], (1, 3, 2, 0, 4, 5)).reshape(ny, block, width)
    grad_b = jnp.transpose(grad[1], (3, 1, 2, 0, 4, 5)).reshape(nx, block, width)

    parts_a = []
    parts_b = []
    for rows_a, rows_b, pick in (
        (stage_a, stage_b, [0]),
        (near_a, near_b, [1, 3]),
        (final_a[2], final_b[2], [2]),
    ):
        cot_a = jnp.concatenate([grad_a[k] for k in pick], axis=0)
        cot_b = jnp.concatenate([grad_b[k] for k in pick], axis=0)
        parts_a.append(chunk_pass(rows_a, gate_weight[0], up_weight[0], cot_a))
        parts_b.append(chunk_pass(rows_b, gate_weight[1], up_weight[1], cot_b))

    def assemble(parts, lead, nxt):
        own, near, far = (p[0] for p in parts)
        plus, minus = near[:block], near[block:]
        rows = jnp.concatenate([own, plus, far, minus], axis=0)
        grads = [sum(p[i] for p in parts) for i in (1, 2)]
        return rows.reshape(lead, nxt, nz, owners, CAP, width), grads

    hid_a, (g_a, u_a) = assemble(parts_a, ny, nx)
    hid_b, (g_b, u_b) = assemble(parts_b, nx, ny)
    back_y = (jnp.arange(ny) - py) % ny
    back_z = (jnp.arange(nz) - pz) % nz
    back_x = (jnp.arange(nx) - px) % nx
    iy = back_y[:, None, None]
    iz = back_z[None, :, None]
    ix = back_x[None, None, :]
    abs_a = hid_a[iy, ix, iz]
    abs_b = hid_b[ix, iy, iz]
    hidden = jnp.stack([abs_a, abs_b], axis=0)
    hidden = jnp.transpose(hidden, (0, 4, 1, 2, 3, 5, 6)).reshape(hidden_grad.shape)
    gate_grad = jnp.stack([g_a, g_b], axis=0)
    up_grad = jnp.stack([u_a, u_b], axis=0)
    return (hidden, gate_grad, up_grad)


def solution(mesh):
    grid = Mesh(mesh.devices.reshape(mesh.shape["expert"], 4, 2, -1), ("expert",) + FSDP_AXES)
    rows_spec = P(("expert",) + FSDP_AXES, None)
    expert_spec = P("expert", None, FSDP_AXES)
    in_specs = (rows_spec, rows_spec, expert_spec, expert_spec, expert_spec)
    out_specs = (expert_spec, expert_spec, expert_spec)
    return jax.shard_map(
        on_device, mesh=grid, in_specs=in_specs, out_specs=out_specs, check_vma=False
    )
```

```python
import jax
import jax.numpy as jnp
from jax import lax
from jax.sharding import Mesh
from jax.sharding import PartitionSpec as P

CAP = 24
FSDP_AXES = ("y", "zh", "x")


def shift(value, axis, step):
    size = lax.axis_size(axis)
    return lax.ppermute(value, axis, [(j, (j + step) % size) for j in range(size)])


def paired_ring(first, first_axis, second, second_axis):
    first_minus = shift(first, first_axis, 1)
    first_plus = shift(first, first_axis, -1)
    second_minus = shift(second, second_axis, 1)
    second_plus = shift(second, second_axis, -1)
    first_minus, first_plus, second_minus, second_plus = lax.optimization_barrier(
        (first_minus, first_plus, second_minus, second_plus)
    )
    half = first.shape[0] // 2

    def far(minus, plus, axis):
        return shift(minus[:half], axis, 1), shift(plus[half:], axis, -1)

    first_lo, first_hi = far(first_minus, first_plus, first_axis)
    second_lo, second_hi = far(second_minus, second_plus, second_axis)
    first_lo, first_hi, second_lo, second_hi = lax.optimization_barrier(
        (first_lo, first_hi, second_lo, second_hi)
    )
    first_far = jnp.concatenate([first_lo, first_hi], axis=0)
    second_far = jnp.concatenate([second_lo, second_hi], axis=0)
    return [first, first_plus, first_far, first_minus], [second, second_plus, second_far, second_minus]


def chunk_pass(rows, gate_w, up_w, cotan):
    gate = jnp.dot(rows, gate_w, preferred_element_type=jnp.float32)
    upval = jnp.dot(rows, up_w, preferred_element_type=jnp.float32)
    cotan = cotan.astype(jnp.float32)
    sigma = 1.0 / (1.0 + jnp.exp(-gate))
    active = gate * sigma
    hidden = (active * upval).astype(jnp.bfloat16)
    gate_delta = (cotan * upval * sigma * (1.0 + gate * (1.0 - sigma))).astype(jnp.bfloat16)
    up_delta = (cotan * active).astype(jnp.bfloat16)
    gate_sum = jnp.dot(rows.T, gate_delta, preferred_element_type=jnp.float32)
    up_sum = jnp.dot(rows.T, up_delta, preferred_element_type=jnp.float32)
    return hidden, gate_sum, up_sum


def batched_pass(rows, gate_w, up_w, cotan, gate_base, up_base):
    gate = jnp.einsum("grd,gdf->grf", rows, gate_w, preferred_element_type=jnp.float32)
    upval = jnp.einsum("grd,gdf->grf", rows, up_w, preferred_element_type=jnp.float32)
    cotan = cotan.astype(jnp.float32)
    sigma = 1.0 / (1.0 + jnp.exp(-gate))
    active = gate * sigma
    hidden = (active * upval).astype(jnp.bfloat16)
    gate_delta = (cotan * upval * sigma * (1.0 + gate * (1.0 - sigma))).astype(jnp.bfloat16)
    up_delta = (cotan * active).astype(jnp.bfloat16)
    gate_sum = gate_base + jnp.einsum(
        "grd,grf->gdf", rows, gate_delta, preferred_element_type=jnp.float32
    )
    up_sum = up_base + jnp.einsum("grd,grf->gdf", rows, up_delta, preferred_element_type=jnp.float32)
    return hidden, gate_sum, up_sum


def on_device(tokens, expert_ids, gate_weight, up_weight, hidden_grad):
    owners = lax.axis_size("expert")
    per_owner = gate_weight.shape[0]
    model = gate_weight.shape[1]
    width = gate_weight.shape[2]
    route = expert_ids[:, 0]
    total_experts = per_owner * owners
    onehot = (route[:, None] == jnp.arange(total_experts, dtype=jnp.int32)[None, :]).astype(
        jnp.int32
    )
    rank = jnp.sum((jnp.cumsum(onehot, axis=0) - onehot) * onehot, axis=1)
    owner_of = route // per_owner
    within = route % per_owner
    target = owner_of * (per_owner * CAP) + within * CAP + rank
    send_rows = per_owner * owners * CAP
    placing = (jnp.arange(send_rows, dtype=jnp.int32)[:, None] == target[None, :]).astype(
        jnp.bfloat16
    )
    outgoing = jnp.dot(placing, tokens, preferred_element_type=jnp.float32).astype(jnp.bfloat16)
    outgoing = outgoing.reshape(owners, per_owner, CAP, model)
    arrived = lax.all_to_all(outgoing, "expert", split_axis=0, concat_axis=0, tiled=True)
    by_expert = jnp.transpose(arrived, (1, 0, 2, 3)).reshape(per_owner, owners * CAP, model)

    ny, nz, nx = (lax.axis_size(a) for a in FSDP_AXES)
    py, pz, px = (lax.axis_index(a) for a in FSDP_AXES)
    local = jnp.stack([by_expert, shift(by_expert, "zh", 1)], axis=1)
    local = local.reshape(per_owner, nz * owners * CAP, model)
    stage_a, stage_b = paired_ring(local[0], "x", local[1], "y")
    stage_a = jnp.concatenate(stage_a, axis=0)
    stage_b = jnp.concatenate(stage_b, axis=0)
    final_a, final_b = paired_ring(stage_a, "y", stage_b, "x")
    near_a = jnp.concatenate([final_a[1], final_a[3]], axis=0)
    near_b = jnp.concatenate([final_b[1], final_b[3]], axis=0)

    grad = hidden_grad.reshape(per_owner, owners, ny, nz, nx, CAP, width)
    grad = jnp.roll(grad, -py, axis=2)
    grad = jnp.roll(grad, -pz, axis=3)
    grad = jnp.roll(grad, -px, axis=4)
    block = nx * nz * owners * CAP
    grad_a = jnp.transpose(grad[0], (1, 3, 2, 0, 4, 5)).reshape(ny, block, width)
    grad_b = jnp.transpose(grad[1], (3, 1, 2, 0, 4, 5)).reshape(nx, block, width)

    parts_a = []
    parts_b = []
    for rows_a, rows_b, pick in ((stage_a, stage_b, [0]), (near_a, near_b, [1, 3])):
        cot_a = jnp.concatenate([grad_a[k] for k in pick], axis=0)
        cot_b = jnp.concatenate([grad_b[k] for k in pick], axis=0)
        parts_a.append(chunk_pass(rows_a, gate_weight[0], up_weight[0], cot_a))
        parts_b.append(chunk_pass(rows_b, gate_weight[1], up_weight[1], cot_b))
    gate_base = jnp.stack([parts_a[0][1] + parts_a[1][1], parts_b[0][1] + parts_b[1][1]])
    up_base = jnp.stack([parts_a[0][2] + parts_a[1][2], parts_b[0][2] + parts_b[1][2]])
    far_rows = jnp.stack([final_a[2], final_b[2]])
    far_cot = jnp.stack([grad_a[2], grad_b[2]])
    far_hidden, gate_grad, up_grad = batched_pass(
        far_rows, gate_weight, up_weight, far_cot, gate_base, up_base
    )

    def assemble(parts, far, lead, nxt):
        own, near = (p[0] for p in parts)
        plus, minus = near[:block], near[block:]
        rows = jnp.concatenate([own, plus, far, minus], axis=0)
        return rows.reshape(lead, nxt, nz, owners, CAP, width)

    hid_a = assemble(parts_a, far_hidden[0], ny, nx)
    hid_b = assemble(parts_b, far_hidden[1], nx, ny)
    hidden = jnp.stack(
        [jnp.transpose(hid_a, (3, 0, 2, 1, 4, 5)), jnp.transpose(hid_b, (3, 1, 2, 0, 4, 5))], axis=0
    )
    hidden = jnp.roll(hidden, py, axis=2)
    hidden = jnp.roll(hidden, pz, axis=3)
    hidden = jnp.roll(hidden, px, axis=4)
    hidden = hidden.reshape(hidden_grad.shape)
    return (hidden, gate_grad, up_grad)


def solution(mesh):
    grid = Mesh(mesh.devices.reshape(mesh.shape["expert"], 4, 2, -1), ("expert",) + FSDP_AXES)
    rows_spec = P(("expert",) + FSDP_AXES, None)
    expert_spec = P("expert", None, FSDP_AXES)
    in_specs = (rows_spec, rows_spec, expert_spec, expert_spec, expert_spec)
    out_specs = (expert_spec, expert_spec, expert_spec)
    return jax.shard_map(
        on_device, mesh=grid, in_specs=in_specs, out_specs=out_specs, check_vma=False
    )
```

```python
import jax
import jax.numpy as jnp
from jax import lax
from jax.sharding import Mesh
from jax.sharding import PartitionSpec as P

CAP = 24
FSDP_AXES = ("y", "zh", "x")


def shift(value, axis, step):
    size = lax.axis_size(axis)
    return lax.ppermute(value, axis, [(j, (j + step) % size) for j in range(size)])


def paired_ring(first, first_axis, second, second_axis):
    first_minus = shift(first, first_axis, 1)
    first_plus = shift(first, first_axis, -1)
    second_minus = shift(second, second_axis, 1)
    second_plus = shift(second, second_axis, -1)
    first_minus, first_plus, second_minus, second_plus = lax.optimization_barrier(
        (first_minus, first_plus, second_minus, second_plus)
    )
    half = first.shape[0] // 2

    def far(minus, plus, axis):
        return shift(minus[:half], axis, 1), shift(plus[half:], axis, -1)

    first_lo, first_hi = far(first_minus, first_plus, first_axis)
    second_lo, second_hi = far(second_minus, second_plus, second_axis)
    first_lo, first_hi, second_lo, second_hi = lax.optimization_barrier(
        (first_lo, first_hi, second_lo, second_hi)
    )
    first_far = jnp.concatenate([first_lo, first_hi], axis=0)
    second_far = jnp.concatenate([second_lo, second_hi], axis=0)
    return [first, first_plus, first_far, first_minus], [second, second_plus, second_far, second_minus]


def chunk_pass(rows, both_w, cotan):
    width = cotan.shape[-1]
    both = jnp.dot(rows, both_w, preferred_element_type=jnp.float32)
    gate = both[:, :width]
    upval = both[:, width:]
    cotan = cotan.astype(jnp.float32)
    sigma = 1.0 / (1.0 + jnp.exp(-gate))
    active = gate * sigma
    hidden = (active * upval).astype(jnp.bfloat16)
    gate_delta = (cotan * upval * sigma * (1.0 + gate * (1.0 - sigma))).astype(jnp.bfloat16)
    up_delta = (cotan * active).astype(jnp.bfloat16)
    deltas = jnp.concatenate([gate_delta, up_delta], axis=1)
    return hidden, jnp.dot(rows.T, deltas, preferred_element_type=jnp.float32)


def on_device(tokens, expert_ids, gate_weight, up_weight, hidden_grad):
    owners = lax.axis_size("expert")
    per_owner = gate_weight.shape[0]
    model = gate_weight.shape[1]
    width = gate_weight.shape[2]
    route = expert_ids[:, 0]
    total_experts = per_owner * owners
    onehot = (route[:, None] == jnp.arange(total_experts, dtype=jnp.int32)[None, :]).astype(
        jnp.int32
    )
    rank = jnp.sum((jnp.cumsum(onehot, axis=0) - onehot) * onehot, axis=1)
    owner_of = route // per_owner
    within = route % per_owner
    target = owner_of * (per_owner * CAP) + within * CAP + rank
    send_rows = per_owner * owners * CAP
    placing = (jnp.arange(send_rows, dtype=jnp.int32)[:, None] == target[None, :]).astype(
        jnp.bfloat16
    )
    outgoing = jnp.dot(placing, tokens, preferred_element_type=jnp.float32).astype(jnp.bfloat16)
    outgoing = outgoing.reshape(owners, per_owner, CAP, model)
    arrived = lax.all_to_all(outgoing, "expert", split_axis=0, concat_axis=0, tiled=True)
    by_expert = jnp.transpose(arrived, (1, 0, 2, 3)).reshape(per_owner, owners * CAP, model)

    ny, nz, nx = (lax.axis_size(a) for a in FSDP_AXES)
    py, pz, px = (lax.axis_index(a) for a in FSDP_AXES)
    local = jnp.stack([by_expert, shift(by_expert, "zh", 1)], axis=1)
    local = local.reshape(per_owner, nz * owners * CAP, model)
    stage_a, stage_b = paired_ring(local[0], "x", local[1], "y")
    stage_a = jnp.concatenate(stage_a, axis=0)
    stage_b = jnp.concatenate(stage_b, axis=0)
    final_a, final_b = paired_ring(stage_a, "y", stage_b, "x")
    near_a = jnp.concatenate([final_a[1], final_a[3]], axis=0)
    near_b = jnp.concatenate([final_b[1], final_b[3]], axis=0)

    grad = hidden_grad.reshape(per_owner, owners, ny, nz, nx, CAP, width)
    grad = jnp.roll(grad, -py, axis=2)
    grad = jnp.roll(grad, -pz, axis=3)
    grad = jnp.roll(grad, -px, axis=4)
    block = nx * nz * owners * CAP
    grad_a = jnp.transpose(grad[0], (1, 3, 2, 0, 4, 5)).reshape(ny, block, width)
    grad_b = jnp.transpose(grad[1], (3, 1, 2, 0, 4, 5)).reshape(nx, block, width)

    both_a = jnp.concatenate([gate_weight[0], up_weight[0]], axis=1)
    both_b = jnp.concatenate([gate_weight[1], up_weight[1]], axis=1)
    parts_a = []
    parts_b = []
    for rows_a, rows_b, pick in (
        (stage_a, stage_b, [0]),
        (near_a, near_b, [1, 3]),
        (final_a[2], final_b[2], [2]),
    ):
        cot_a = jnp.concatenate([grad_a[k] for k in pick], axis=0)
        cot_b = jnp.concatenate([grad_b[k] for k in pick], axis=0)
        parts_a.append(chunk_pass(rows_a, both_a, cot_a))
        parts_b.append(chunk_pass(rows_b, both_b, cot_b))

    def assemble(parts, lead, nxt):
        own, near, far = (p[0] for p in parts)
        plus, minus = near[:block], near[block:]
        rows = jnp.concatenate([own, plus, far, minus], axis=0)
        total = parts[0][1] + parts[1][1] + parts[2][1]
        return rows.reshape(lead, nxt, nz, owners, CAP, width), total

    hid_a, grad_sum_a = assemble(parts_a, ny, nx)
    hid_b, grad_sum_b = assemble(parts_b, nx, ny)
    hidden = jnp.stack(
        [jnp.transpose(hid_a, (3, 0, 2, 1, 4, 5)), jnp.transpose(hid_b, (3, 1, 2, 0, 4, 5))], axis=0
    )
    hidden = jnp.roll(hidden, py, axis=2)
    hidden = jnp.roll(hidden, pz, axis=3)
    hidden = jnp.roll(hidden, px, axis=4)
    hidden = hidden.reshape(hidden_grad.shape)
    gate_grad = jnp.stack([grad_sum_a[:, :width], grad_sum_b[:, :width]], axis=0)
    up_grad = jnp.stack([grad_sum_a[:, width:], grad_sum_b[:, width:]], axis=0)
    return (hidden, gate_grad, up_grad)


def solution(mesh):
    grid = Mesh(mesh.devices.reshape(mesh.shape["expert"], 4, 2, -1), ("expert",) + FSDP_AXES)
    rows_spec = P(("expert",) + FSDP_AXES, None)
    expert_spec = P("expert", None, FSDP_AXES)
    in_specs = (rows_spec, rows_spec, expert_spec, expert_spec, expert_spec)
    out_specs = (expert_spec, expert_spec, expert_spec)
    return jax.shard_map(
        on_device, mesh=grid, in_specs=in_specs, out_specs=out_specs, check_vma=False
    )
```

```python
import jax
import jax.numpy as jnp
from jax import lax
from jax.sharding import Mesh
from jax.sharding import PartitionSpec as P

CAP = 24
FSDP_AXES = ("y", "zh", "x")


def shift(value, axis, step):
    size = lax.axis_size(axis)
    return lax.ppermute(value, axis, [(j, (j + step) % size) for j in range(size)])


def place(pieces, position):
    count = len(pieces)
    rows = pieces[0].shape[0]
    out = jnp.zeros((count * rows,) + pieces[0].shape[1:], pieces[0].dtype)
    for offset, piece in enumerate(pieces):
        start = ((position + offset) % count) * rows
        out = lax.dynamic_update_slice_in_dim(out, piece, start, axis=0)
    return out


def paired_ring(first, first_axis, second, second_axis):
    first_minus = shift(first, first_axis, 1)
    first_plus = shift(first, first_axis, -1)
    second_minus = shift(second, second_axis, 1)
    second_plus = shift(second, second_axis, -1)
    first_minus, first_plus, second_minus, second_plus = lax.optimization_barrier(
        (first_minus, first_plus, second_minus, second_plus)
    )
    half = first.shape[0] // 2

    def far(minus, plus, axis):
        return shift(minus[:half], axis, 1), shift(plus[half:], axis, -1)

    first_lo, first_hi = far(first_minus, first_plus, first_axis)
    second_lo, second_hi = far(second_minus, second_plus, second_axis)
    first_lo, first_hi, second_lo, second_hi = lax.optimization_barrier(
        (first_lo, first_hi, second_lo, second_hi)
    )
    first_far = jnp.concatenate([first_lo, first_hi], axis=0)
    second_far = jnp.concatenate([second_lo, second_hi], axis=0)
    return [first, first_plus, first_far, first_minus], [second, second_plus, second_far, second_minus]


def chunk_pass(rows, gate_w, up_w, cotan):
    gate = jnp.dot(rows, gate_w, preferred_element_type=jnp.float32)
    upval = jnp.dot(rows, up_w, preferred_element_type=jnp.float32)
    cotan = cotan.astype(jnp.float32)
    sigma = 1.0 / (1.0 + jnp.exp(-gate))
    active = gate * sigma
    hidden = (active * upval).astype(jnp.bfloat16)
    gate_delta = (cotan * upval * sigma * (1.0 + gate * (1.0 - sigma))).astype(jnp.bfloat16)
    up_delta = (cotan * active).astype(jnp.bfloat16)
    gate_sum = jnp.dot(rows.T, gate_delta, preferred_element_type=jnp.float32)
    up_sum = jnp.dot(rows.T, up_delta, preferred_element_type=jnp.float32)
    return hidden, gate_sum, up_sum


def on_device(tokens, expert_ids, gate_weight, up_weight, hidden_grad):
    owners = lax.axis_size("expert")
    per_owner = gate_weight.shape[0]
    model = gate_weight.shape[1]
    width = gate_weight.shape[2]
    route = expert_ids[:, 0]
    total_experts = per_owner * owners
    onehot = (route[:, None] == jnp.arange(total_experts, dtype=jnp.int32)[None, :]).astype(
        jnp.int32
    )
    rank = jnp.sum((jnp.cumsum(onehot, axis=0) - onehot) * onehot, axis=1)
    owner_of = route // per_owner
    within = route % per_owner
    target = owner_of * (per_owner * CAP) + within * CAP + rank
    send_rows = per_owner * owners * CAP
    placing = (jnp.arange(send_rows, dtype=jnp.int32)[:, None] == target[None, :]).astype(
        jnp.bfloat16
    )
    outgoing = jnp.dot(placing, tokens, preferred_element_type=jnp.float32).astype(jnp.bfloat16)
    outgoing = outgoing.reshape(owners, per_owner, CAP, model)
    arrived = lax.all_to_all(outgoing, "expert", split_axis=0, concat_axis=0, tiled=True)
    by_expert = jnp.transpose(arrived, (1, 0, 2, 3)).reshape(per_owner, owners * CAP, model)

    ny, nz, nx = (lax.axis_size(a) for a in FSDP_AXES)
    py, pz, px = (lax.axis_index(a) for a in FSDP_AXES)
    partner = shift(by_expert, "zh", 1)
    local = [place([by_expert[g], partner[g]], pz) for g in range(per_owner)]
    stage_a, stage_b = paired_ring(local[0], "x", local[1], "y")
    stage_a = place(stage_a, px)
    stage_b = place(stage_b, py)
    final_a, final_b = paired_ring(stage_a, "y", stage_b, "x")
    near_a = jnp.concatenate([final_a[1], final_a[3]], axis=0)
    near_b = jnp.concatenate([final_b[1], final_b[3]], axis=0)

    grad = hidden_grad.reshape(per_owner, owners, ny, nz, nx, CAP, width)
    block = nx * nz * owners * CAP
    grad_a = jnp.transpose(grad[0], (1, 3, 2, 0, 4, 5)).reshape(ny, block, width)
    grad_b = jnp.transpose(grad[1], (3, 1, 2, 0, 4, 5)).reshape(nx, block, width)

    def pick(table, position, offsets):
        size = table.shape[0]
        return jnp.concatenate(
            [lax.dynamic_index_in_dim(table, (position + k) % size, 0, keepdims=False) for k in offsets],
            axis=0,
        )

    parts_a = []
    parts_b = []
    for rows_a, rows_b, offsets in (
        (stage_a, stage_b, [0]),
        (near_a, near_b, [1, 3]),
        (final_a[2], final_b[2], [2]),
    ):
        parts_a.append(chunk_pass(rows_a, gate_weight[0], up_weight[0], pick(grad_a, py, offsets)))
        parts_b.append(chunk_pass(rows_b, gate_weight[1], up_weight[1], pick(grad_b, px, offsets)))

    def assemble(parts, position, lead, nxt):
        own, near, far = (p[0] for p in parts)
        plus, minus = near[:block], near[block:]
        rows = place([own, plus, far, minus], position)
        grads = [sum(p[i] for p in parts) for i in (1, 2)]
        return rows.reshape(lead, nxt, nz, owners, CAP, width), grads

    hid_a, (g_a, u_a) = assemble(parts_a, py, ny, nx)
    hid_b, (g_b, u_b) = assemble(parts_b, px, nx, ny)
    hidden = jnp.stack(
        [jnp.transpose(hid_a, (3, 0, 2, 1, 4, 5)), jnp.transpose(hid_b, (3, 1, 2, 0, 4, 5))], axis=0
    )
    hidden = hidden.reshape(hidden_grad.shape)
    gate_grad = jnp.stack([g_a, g_b], axis=0)
    up_grad = jnp.stack([u_a, u_b], axis=0)
    return (hidden, gate_grad, up_grad)


def solution(mesh):
    grid = Mesh(mesh.devices.reshape(mesh.shape["expert"], 4, 2, -1), ("expert",) + FSDP_AXES)
    rows_spec = P(("expert",) + FSDP_AXES, None)
    expert_spec = P("expert", None, FSDP_AXES)
    in_specs = (rows_spec, rows_spec, expert_spec, expert_spec, expert_spec)
    out_specs = (expert_spec, expert_spec, expert_spec)
    return jax.shard_map(
        on_device, mesh=grid, in_specs=in_specs, out_specs=out_specs, check_vma=False
    )
```

```python
import jax
import jax.numpy as jnp
from jax import lax
from jax.sharding import Mesh
from jax.sharding import PartitionSpec as P

CAP = 24
FSDP_AXES = ("y", "zh", "x")


def shift(value, axis, step):
    size = lax.axis_size(axis)
    return lax.ppermute(value, axis, [(j, (j + step) % size) for j in range(size)])


def place(pieces, position):
    count = len(pieces)
    rows = pieces[0].shape[0]
    out = jnp.zeros((count * rows,) + pieces[0].shape[1:], pieces[0].dtype)
    for offset, piece in enumerate(pieces):
        start = ((position + offset) % count) * rows
        out = lax.dynamic_update_slice_in_dim(out, piece, start, axis=0)
    return out


def paired_ring(first, first_axis, second, second_axis):
    first_minus = shift(first, first_axis, 1)
    first_plus = shift(first, first_axis, -1)
    second_minus = shift(second, second_axis, 1)
    second_plus = shift(second, second_axis, -1)
    first_minus, first_plus, second_minus, second_plus = lax.optimization_barrier(
        (first_minus, first_plus, second_minus, second_plus)
    )
    half = first.shape[0] // 2

    def far(minus, plus, axis):
        return shift(minus[:half], axis, 1), shift(plus[half:], axis, -1)

    first_lo, first_hi = far(first_minus, first_plus, first_axis)
    second_lo, second_hi = far(second_minus, second_plus, second_axis)
    first_lo, first_hi, second_lo, second_hi = lax.optimization_barrier(
        (first_lo, first_hi, second_lo, second_hi)
    )
    first_far = jnp.concatenate([first_lo, first_hi], axis=0)
    second_far = jnp.concatenate([second_lo, second_hi], axis=0)
    return [first, first_plus, first_far, first_minus], [second, second_plus, second_far, second_minus]


def chunk_pass(rows, gate_w, up_w, cotan):
    gate = jnp.dot(rows, gate_w, preferred_element_type=jnp.float32)
    upval = jnp.dot(rows, up_w, preferred_element_type=jnp.float32)
    cotan = cotan.astype(jnp.float32)
    sigma = 1.0 / (1.0 + jnp.exp(-gate))
    active = gate * sigma
    hidden = (active * upval).astype(jnp.bfloat16)
    gate_delta = (cotan * upval * sigma * (1.0 + gate * (1.0 - sigma))).astype(jnp.bfloat16)
    up_delta = (cotan * active).astype(jnp.bfloat16)
    gate_sum = jnp.dot(rows.T, gate_delta, preferred_element_type=jnp.float32)
    up_sum = jnp.dot(rows.T, up_delta, preferred_element_type=jnp.float32)
    return hidden, gate_sum, up_sum


def on_device(tokens, expert_ids, gate_weight, up_weight, hidden_grad):
    owners = lax.axis_size("expert")
    per_owner = gate_weight.shape[0]
    model = gate_weight.shape[1]
    width = gate_weight.shape[2]
    route = expert_ids[:, 0]
    total_experts = per_owner * owners
    onehot = (route[:, None] == jnp.arange(total_experts, dtype=jnp.int32)[None, :]).astype(
        jnp.int32
    )
    rank = jnp.sum((jnp.cumsum(onehot, axis=0) - onehot) * onehot, axis=1)
    owner_of = route // per_owner
    within = route % per_owner
    target = owner_of * (per_owner * CAP) + within * CAP + rank
    send_rows = per_owner * owners * CAP
    placing = (jnp.arange(send_rows, dtype=jnp.int32)[:, None] == target[None, :]).astype(
        jnp.bfloat16
    )
    outgoing = jnp.dot(placing, tokens, preferred_element_type=jnp.float32).astype(jnp.bfloat16)
    outgoing = outgoing.reshape(owners, per_owner, CAP, model)
    arrived = lax.all_to_all(outgoing, "expert", split_axis=0, concat_axis=0, tiled=True)
    by_expert = jnp.transpose(arrived, (1, 0, 2, 3)).reshape(per_owner, owners * CAP, model)

    ny, nz, nx = (lax.axis_size(a) for a in FSDP_AXES)
    py, pz, px = (lax.axis_index(a) for a in FSDP_AXES)
    partner = shift(by_expert, "zh", 1)
    local = [place([by_expert[g], partner[g]], pz) for g in range(per_owner)]
    stage_a, stage_b = paired_ring(local[0], "x", local[1], "y")
    stage_a = place(stage_a, px)
    stage_b = place(stage_b, py)
    final_a, final_b = paired_ring(stage_a, "y", stage_b, "x")
    near_a = jnp.concatenate([final_a[1], final_a[3]], axis=0)
    near_b = jnp.concatenate([final_b[1], final_b[3]], axis=0)

    grad = hidden_grad.reshape(per_owner, owners, ny, nz, nx, CAP, width)
    block = nx * nz * owners * CAP
    grad_a = jnp.transpose(grad[0], (1, 3, 2, 0, 4, 5)).reshape(ny, block, width)
    grad_b = jnp.transpose(grad[1], (3, 1, 2, 0, 4, 5)).reshape(nx, block, width)

    grad_a = jnp.roll(grad_a, -py, axis=0)
    grad_b = jnp.roll(grad_b, -px, axis=0)

    def pick(table, offsets):
        return jnp.concatenate([table[k] for k in offsets], axis=0)

    parts_a = []
    parts_b = []
    for rows_a, rows_b, offsets in (
        (stage_a, stage_b, [0]),
        (near_a, near_b, [1, 3]),
        (final_a[2], final_b[2], [2]),
    ):
        parts_a.append(chunk_pass(rows_a, gate_weight[0], up_weight[0], pick(grad_a, offsets)))
        parts_b.append(chunk_pass(rows_b, gate_weight[1], up_weight[1], pick(grad_b, offsets)))

    def assemble(parts, position, lead, nxt):
        own, near, far = (p[0] for p in parts)
        plus, minus = near[:block], near[block:]
        rows = place([own, plus, far, minus], position)
        grads = [sum(p[i] for p in parts) for i in (1, 2)]
        return rows.reshape(lead, nxt, nz, owners, CAP, width), grads

    hid_a, (g_a, u_a) = assemble(parts_a, py, ny, nx)
    hid_b, (g_b, u_b) = assemble(parts_b, px, nx, ny)
    hidden = jnp.stack(
        [jnp.transpose(hid_a, (3, 0, 2, 1, 4, 5)), jnp.transpose(hid_b, (3, 1, 2, 0, 4, 5))], axis=0
    )
    hidden = hidden.reshape(hidden_grad.shape)
    gate_grad = jnp.stack([g_a, g_b], axis=0)
    up_grad = jnp.stack([u_a, u_b], axis=0)
    return (hidden, gate_grad, up_grad)


def solution(mesh):
    grid = Mesh(mesh.devices.reshape(mesh.shape["expert"], 4, 2, -1), ("expert",) + FSDP_AXES)
    rows_spec = P(("expert",) + FSDP_AXES, None)
    expert_spec = P("expert", None, FSDP_AXES)
    in_specs = (rows_spec, rows_spec, expert_spec, expert_spec, expert_spec)
    out_specs = (expert_spec, expert_spec, expert_spec)
    return jax.shard_map(
        on_device, mesh=grid, in_specs=in_specs, out_specs=out_specs, check_vma=False
    )
```

```python
import jax
import jax.numpy as jnp
from jax import lax
from jax.sharding import Mesh
from jax.sharding import PartitionSpec as P

CAP = 24
FSDP_AXES = ("y", "zh", "x")


def shift(value, axis, step):
    size = lax.axis_size(axis)
    return lax.ppermute(value, axis, [(j, (j + step) % size) for j in range(size)])


def paired_ring(first, first_axis, second, second_axis):
    first_minus = shift(first, first_axis, 1)
    first_plus = shift(first, first_axis, -1)
    second_minus = shift(second, second_axis, 1)
    second_plus = shift(second, second_axis, -1)
    first_minus, first_plus, second_minus, second_plus = lax.optimization_barrier(
        (first_minus, first_plus, second_minus, second_plus)
    )
    half = first.shape[0] // 2

    def far(minus, plus, axis):
        return shift(minus[:half], axis, 1), shift(plus[half:], axis, -1)

    first_lo, first_hi = far(first_minus, first_plus, first_axis)
    second_lo, second_hi = far(second_minus, second_plus, second_axis)
    first_lo, first_hi, second_lo, second_hi = lax.optimization_barrier(
        (first_lo, first_hi, second_lo, second_hi)
    )
    first_far = jnp.concatenate([first_lo, first_hi], axis=0)
    second_far = jnp.concatenate([second_lo, second_hi], axis=0)
    return [first, first_plus, first_far, first_minus], [second, second_plus, second_far, second_minus]


def chunk_pass(rows, gate_w, up_w, cotan):
    gate = jnp.dot(rows, gate_w, preferred_element_type=jnp.float32)
    upval = jnp.dot(rows, up_w, preferred_element_type=jnp.float32)
    cotan = cotan.astype(jnp.float32)
    sigma = 1.0 / (1.0 + jnp.exp(-gate))
    active = gate * sigma
    hidden = (active * upval).astype(jnp.bfloat16)
    gate_delta = (cotan * upval * sigma * (1.0 + gate * (1.0 - sigma))).astype(jnp.bfloat16)
    up_delta = (cotan * active).astype(jnp.bfloat16)
    gate_sum = jnp.dot(rows.T, gate_delta, preferred_element_type=jnp.float32)
    up_sum = jnp.dot(rows.T, up_delta, preferred_element_type=jnp.float32)
    return hidden, gate_sum, up_sum


def on_device(tokens, expert_ids, gate_weight, up_weight, hidden_grad):
    owners = lax.axis_size("expert")
    per_owner = gate_weight.shape[0]
    model = gate_weight.shape[1]
    width = gate_weight.shape[2]
    route = expert_ids[:, 0]
    total_experts = per_owner * owners
    onehot = (route[:, None] == jnp.arange(total_experts, dtype=jnp.int32)[None, :]).astype(
        jnp.int32
    )
    rank = jnp.sum((jnp.cumsum(onehot, axis=0) - onehot) * onehot, axis=1)
    owner_of = route // per_owner
    within = route % per_owner
    target = owner_of * (per_owner * CAP) + within * CAP + rank
    send_rows = per_owner * owners * CAP
    placing = (jnp.arange(send_rows, dtype=jnp.int32)[:, None] == target[None, :]).astype(
        jnp.bfloat16
    )
    outgoing = jnp.dot(placing, tokens, preferred_element_type=jnp.float32).astype(jnp.bfloat16)
    outgoing = outgoing.reshape(owners, per_owner, CAP, model)
    partner_out = shift(outgoing, "zh", 1)
    arrived = lax.all_to_all(outgoing, "expert", split_axis=0, concat_axis=0, tiled=True)
    arrived_p = lax.all_to_all(partner_out, "expert", split_axis=0, concat_axis=0, tiled=True)
    by_expert = jnp.transpose(arrived, (1, 0, 2, 3)).reshape(per_owner, owners * CAP, model)
    partner = jnp.transpose(arrived_p, (1, 0, 2, 3)).reshape(per_owner, owners * CAP, model)

    ny, nz, nx = (lax.axis_size(a) for a in FSDP_AXES)
    py, pz, px = (lax.axis_index(a) for a in FSDP_AXES)
    local = jnp.stack([by_expert, partner], axis=1)
    local = local.reshape(per_owner, nz * owners * CAP, model)
    stage_a, stage_b = paired_ring(local[0], "x", local[1], "y")
    stage_a = jnp.concatenate(stage_a, axis=0)
    stage_b = jnp.concatenate(stage_b, axis=0)
    final_a, final_b = paired_ring(stage_a, "y", stage_b, "x")
    near_a = jnp.concatenate([final_a[1], final_a[3]], axis=0)
    near_b = jnp.concatenate([final_b[1], final_b[3]], axis=0)

    grad = hidden_grad.reshape(per_owner, owners, ny, nz, nx, CAP, width)
    grad = jnp.roll(grad, -py, axis=2)
    grad = jnp.roll(grad, -pz, axis=3)
    grad = jnp.roll(grad, -px, axis=4)
    block = nx * nz * owners * CAP
    grad_a = jnp.transpose(grad[0], (1, 3, 2, 0, 4, 5)).reshape(ny, block, width)
    grad_b = jnp.transpose(grad[1], (3, 1, 2, 0, 4, 5)).reshape(nx, block, width)

    parts_a = []
    parts_b = []
    for rows_a, rows_b, pick in (
        (stage_a, stage_b, [0]),
        (near_a, near_b, [1, 3]),
        (final_a[2], final_b[2], [2]),
    ):
        cot_a = jnp.concatenate([grad_a[k] for k in pick], axis=0)
        cot_b = jnp.concatenate([grad_b[k] for k in pick], axis=0)
        parts_a.append(chunk_pass(rows_a, gate_weight[0], up_weight[0], cot_a))
        parts_b.append(chunk_pass(rows_b, gate_weight[1], up_weight[1], cot_b))

    def assemble(parts, lead, nxt):
        own, near, far = (p[0] for p in parts)
        plus, minus = near[:block], near[block:]
        rows = jnp.concatenate([own, plus, far, minus], axis=0)
        grads = [sum(p[i] for p in parts) for i in (1, 2)]
        return rows.reshape(lead, nxt, nz, owners, CAP, width), grads

    hid_a, (g_a, u_a) = assemble(parts_a, ny, nx)
    hid_b, (g_b, u_b) = assemble(parts_b, nx, ny)
    hidden = jnp.stack(
        [jnp.transpose(hid_a, (3, 0, 2, 1, 4, 5)), jnp.transpose(hid_b, (3, 1, 2, 0, 4, 5))], axis=0
    )
    hidden = jnp.roll(hidden, py, axis=2)
    hidden = jnp.roll(hidden, pz, axis=3)
    hidden = jnp.roll(hidden, px, axis=4)
    hidden = hidden.reshape(hidden_grad.shape)
    gate_grad = jnp.stack([g_a, g_b], axis=0)
    up_grad = jnp.stack([u_a, u_b], axis=0)
    return (hidden, gate_grad, up_grad)


def solution(mesh):
    grid = Mesh(mesh.devices.reshape(mesh.shape["expert"], 4, 2, -1), ("expert",) + FSDP_AXES)
    rows_spec = P(("expert",) + FSDP_AXES, None)
    expert_spec = P("expert", None, FSDP_AXES)
    in_specs = (rows_spec, rows_spec, expert_spec, expert_spec, expert_spec)
    out_specs = (expert_spec, expert_spec, expert_spec)
    return jax.shard_map(
        on_device, mesh=grid, in_specs=in_specs, out_specs=out_specs, check_vma=False
    )
```

```python
import jax
import jax.numpy as jnp
from jax import lax
from jax.sharding import Mesh
from jax.sharding import PartitionSpec as P

CAP = 24
FSDP_AXES = ("y", "zh", "x")


def shift(value, axis, step):
    size = lax.axis_size(axis)
    return lax.ppermute(value, axis, [(j, (j + step) % size) for j in range(size)])


def paired_ring(first, first_axis, second, second_axis):
    first_minus = shift(first, first_axis, 1)
    first_plus = shift(first, first_axis, -1)
    second_minus = shift(second, second_axis, 1)
    second_plus = shift(second, second_axis, -1)
    first_minus, first_plus, second_minus, second_plus = lax.optimization_barrier(
        (first_minus, first_plus, second_minus, second_plus)
    )
    half = first.shape[0] // 2

    def far(minus, plus, axis):
        return shift(minus[:half], axis, 1), shift(plus[half:], axis, -1)

    first_lo, first_hi = far(first_minus, first_plus, first_axis)
    second_lo, second_hi = far(second_minus, second_plus, second_axis)
    first_lo, first_hi, second_lo, second_hi = lax.optimization_barrier(
        (first_lo, first_hi, second_lo, second_hi)
    )
    first_far = jnp.concatenate([first_lo, first_hi], axis=0)
    second_far = jnp.concatenate([second_lo, second_hi], axis=0)
    return [first, first_plus, first_far, first_minus], [second, second_plus, second_far, second_minus]


def paired_ring_halves(first, first_axis, second, second_axis):
    sent = []
    for (lo, hi), axis in ((first, first_axis), (second, second_axis)):
        sent.append([shift(lo, axis, 1), shift(lo, axis, -1), shift(hi, axis, 1), shift(hi, axis, -1)])
    sent = lax.optimization_barrier(sent)
    far = [(shift(m_lo, axis, 1), shift(p_hi, axis, -1))
           for (m_lo, _, _, p_hi), axis in zip(sent, (first_axis, second_axis))]
    far = lax.optimization_barrier(far)
    out = []
    for block, (m_lo, p_lo, m_hi, p_hi), far_pair in zip((first, second), sent, far):
        out.append([block, (p_lo, p_hi), far_pair, (m_lo, m_hi)])
    return out


def chunk_pass(rows, gate_w, up_w, cotan):
    gate = jnp.dot(rows, gate_w, preferred_element_type=jnp.float32)
    upval = jnp.dot(rows, up_w, preferred_element_type=jnp.float32)
    cotan = cotan.astype(jnp.float32)
    sigma = 1.0 / (1.0 + jnp.exp(-gate))
    active = gate * sigma
    hidden = (active * upval).astype(jnp.bfloat16)
    gate_delta = (cotan * upval * sigma * (1.0 + gate * (1.0 - sigma))).astype(jnp.bfloat16)
    up_delta = (cotan * active).astype(jnp.bfloat16)
    gate_sum = jnp.dot(rows.T, gate_delta, preferred_element_type=jnp.float32)
    up_sum = jnp.dot(rows.T, up_delta, preferred_element_type=jnp.float32)
    return hidden, gate_sum, up_sum


def on_device(tokens, expert_ids, gate_weight, up_weight, hidden_grad):
    owners = lax.axis_size("expert")
    per_owner = gate_weight.shape[0]
    model = gate_weight.shape[1]
    width = gate_weight.shape[2]
    route = expert_ids[:, 0]
    total_experts = per_owner * owners
    onehot = (route[:, None] == jnp.arange(total_experts, dtype=jnp.int32)[None, :]).astype(
        jnp.int32
    )
    rank = jnp.sum((jnp.cumsum(onehot, axis=0) - onehot) * onehot, axis=1)
    owner_of = route // per_owner
    within = route % per_owner
    target = owner_of * (per_owner * CAP) + within * CAP + rank
    send_rows = per_owner * owners * CAP
    placing = (jnp.arange(send_rows, dtype=jnp.int32)[:, None] == target[None, :]).astype(
        jnp.bfloat16
    )
    outgoing = jnp.dot(placing, tokens, preferred_element_type=jnp.float32).astype(jnp.bfloat16)
    outgoing = outgoing.reshape(owners, per_owner, CAP, model)
    arrived = lax.all_to_all(outgoing, "expert", split_axis=0, concat_axis=0, tiled=True)
    by_expert = jnp.transpose(arrived, (1, 0, 2, 3)).reshape(per_owner, owners * CAP, model)

    ny, nz, nx = (lax.axis_size(a) for a in FSDP_AXES)
    py, pz, px = (lax.axis_index(a) for a in FSDP_AXES)
    local = jnp.stack([by_expert, shift(by_expert, "zh", 1)], axis=1)
    local = local.reshape(per_owner, nz * owners * CAP, model)
    stage_a, stage_b = paired_ring(local[0], "x", local[1], "y")
    halves_a = (jnp.concatenate(stage_a[:2], axis=0), jnp.concatenate(stage_a[2:], axis=0))
    halves_b = (jnp.concatenate(stage_b[:2], axis=0), jnp.concatenate(stage_b[2:], axis=0))
    final_a, final_b = paired_ring_halves(halves_a, "y", halves_b, "x")
    final_a = [jnp.concatenate(pair, axis=0) for pair in final_a]
    final_b = [jnp.concatenate(pair, axis=0) for pair in final_b]
    stage_a = final_a[0]
    stage_b = final_b[0]
    near_a = jnp.concatenate([final_a[1], final_a[3]], axis=0)
    near_b = jnp.concatenate([final_b[1], final_b[3]], axis=0)

    grad = hidden_grad.reshape(per_owner, owners, ny, nz, nx, CAP, width)
    grad = jnp.roll(grad, -py, axis=2)
    grad = jnp.roll(grad, -pz, axis=3)
    grad = jnp.roll(grad, -px, axis=4)
    block = nx * nz * owners * CAP
    grad_a = jnp.transpose(grad[0], (1, 3, 2, 0, 4, 5)).reshape(ny, block, width)
    grad_b = jnp.transpose(grad[1], (3, 1, 2, 0, 4, 5)).reshape(nx, block, width)

    parts_a = []
    parts_b = []
    for rows_a, rows_b, pick in (
        (stage_a, stage_b, [0]),
        (near_a, near_b, [1, 3]),
        (final_a[2], final_b[2], [2]),
    ):
        cot_a = jnp.concatenate([grad_a[k] for k in pick], axis=0)
        cot_b = jnp.concatenate([grad_b[k] for k in pick], axis=0)
        parts_a.append(chunk_pass(rows_a, gate_weight[0], up_weight[0], cot_a))
        parts_b.append(chunk_pass(rows_b, gate_weight[1], up_weight[1], cot_b))

    def assemble(parts, lead, nxt):
        own, near, far = (p[0] for p in parts)
        plus, minus = near[:block], near[block:]
        rows = jnp.concatenate([own, plus, far, minus], axis=0)
        grads = [sum(p[i] for p in parts) for i in (1, 2)]
        return rows.reshape(lead, nxt, nz, owners, CAP, width), grads

    hid_a, (g_a, u_a) = assemble(parts_a, ny, nx)
    hid_b, (g_b, u_b) = assemble(parts_b, nx, ny)
    hidden = jnp.stack(
        [jnp.transpose(hid_a, (3, 0, 2, 1, 4, 5)), jnp.transpose(hid_b, (3, 1, 2, 0, 4, 5))], axis=0
    )
    hidden = jnp.roll(hidden, py, axis=2)
    hidden = jnp.roll(hidden, pz, axis=3)
    hidden = jnp.roll(hidden, px, axis=4)
    hidden = hidden.reshape(hidden_grad.shape)
    gate_grad = jnp.stack([g_a, g_b], axis=0)
    up_grad = jnp.stack([u_a, u_b], axis=0)
    return (hidden, gate_grad, up_grad)


def solution(mesh):
    grid = Mesh(mesh.devices.reshape(mesh.shape["expert"], 4, 2, -1), ("expert",) + FSDP_AXES)
    rows_spec = P(("expert",) + FSDP_AXES, None)
    expert_spec = P("expert", None, FSDP_AXES)
    in_specs = (rows_spec, rows_spec, expert_spec, expert_spec, expert_spec)
    out_specs = (expert_spec, expert_spec, expert_spec)
    return jax.shard_map(
        on_device, mesh=grid, in_specs=in_specs, out_specs=out_specs, check_vma=False
    )
```

```python
import jax
import jax.numpy as jnp
from jax import lax
from jax.sharding import Mesh
from jax.sharding import PartitionSpec as P

CAP = 24
FSDP_AXES = ("y", "zh", "x")


def shift(value, axis, step):
    size = lax.axis_size(axis)
    return lax.ppermute(value, axis, [(j, (j + step) % size) for j in range(size)])


def paired_ring(first, first_axis, second, second_axis):
    first_minus = shift(first, first_axis, 1)
    first_plus = shift(first, first_axis, -1)
    second_minus = shift(second, second_axis, 1)
    second_plus = shift(second, second_axis, -1)
    first_minus, first_plus, second_minus, second_plus = lax.optimization_barrier(
        (first_minus, first_plus, second_minus, second_plus)
    )
    half = first.shape[0] // 2

    def far(minus, plus, axis):
        return shift(minus[:half], axis, 1), shift(plus[half:], axis, -1)

    first_lo, first_hi = far(first_minus, first_plus, first_axis)
    second_lo, second_hi = far(second_minus, second_plus, second_axis)
    first_lo, first_hi, second_lo, second_hi = lax.optimization_barrier(
        (first_lo, first_hi, second_lo, second_hi)
    )
    first_far = jnp.concatenate([first_lo, first_hi], axis=0)
    second_far = jnp.concatenate([second_lo, second_hi], axis=0)
    return [first, first_plus, first_far, first_minus], [second, second_plus, second_far, second_minus]


def chunk_pass(rows, gate_w, up_w, cotan):
    gate = jnp.dot(rows, gate_w, preferred_element_type=jnp.float32)
    upval = jnp.dot(rows, up_w, preferred_element_type=jnp.float32)
    cotan = cotan.astype(jnp.float32)
    sigma = 1.0 / (1.0 + jnp.exp(-gate))
    active = gate * sigma
    hidden = (active * upval).astype(jnp.bfloat16)
    gate_delta = (cotan * upval * sigma * (1.0 + gate * (1.0 - sigma))).astype(jnp.bfloat16)
    up_delta = (cotan * active).astype(jnp.bfloat16)
    gate_sum = jnp.dot(rows.T, gate_delta, preferred_element_type=jnp.float32)
    up_sum = jnp.dot(rows.T, up_delta, preferred_element_type=jnp.float32)
    return hidden, gate_sum, up_sum


def on_device(tokens, expert_ids, gate_weight, up_weight, hidden_grad):
    owners = lax.axis_size("expert")
    per_owner = gate_weight.shape[0]
    model = gate_weight.shape[1]
    width = gate_weight.shape[2]
    route = expert_ids[:, 0]
    total_experts = per_owner * owners
    onehot = (route[:, None] == jnp.arange(total_experts, dtype=jnp.int32)[None, :]).astype(
        jnp.int32
    )
    rank = jnp.sum((jnp.cumsum(onehot, axis=0) - onehot) * onehot, axis=1)
    owner_of = route // per_owner
    within = route % per_owner
    target = owner_of * (per_owner * CAP) + within * CAP + rank
    send_rows = per_owner * owners * CAP
    placing = (jnp.arange(send_rows, dtype=jnp.int32)[:, None] == target[None, :]).astype(
        jnp.bfloat16
    )
    outgoing = jnp.dot(placing, tokens, preferred_element_type=jnp.float32).astype(jnp.bfloat16)
    outgoing = outgoing.reshape(owners, per_owner, CAP, model)
    arrived = lax.all_to_all(outgoing, "expert", split_axis=0, concat_axis=0, tiled=True)
    by_expert = jnp.transpose(arrived, (1, 0, 2, 3)).reshape(per_owner, owners * CAP, model)

    ny, nz, nx = (lax.axis_size(a) for a in FSDP_AXES)
    py, pz, px = (lax.axis_index(a) for a in FSDP_AXES)
    local = [
        jnp.concatenate([by_expert[g], shift(by_expert[g], "zh", 1)], axis=0) for g in range(per_owner)
    ]
    stage_a, stage_b = paired_ring(local[0], "x", local[1], "y")
    stage_a = jnp.concatenate(stage_a, axis=0)
    stage_b = jnp.concatenate(stage_b, axis=0)
    final_a, final_b = paired_ring(stage_a, "y", stage_b, "x")
    near_a = jnp.concatenate([final_a[1], final_a[3]], axis=0)
    near_b = jnp.concatenate([final_b[1], final_b[3]], axis=0)

    grad = hidden_grad.reshape(per_owner, owners, ny, nz, nx, CAP, width)
    grad = jnp.roll(grad, -py, axis=2)
    grad = jnp.roll(grad, -pz, axis=3)
    grad = jnp.roll(grad, -px, axis=4)
    block = nx * nz * owners * CAP
    grad_a = jnp.transpose(grad[0], (1, 3, 2, 0, 4, 5)).reshape(ny, block, width)
    grad_b = jnp.transpose(grad[1], (3, 1, 2, 0, 4, 5)).reshape(nx, block, width)

    parts_a = []
    parts_b = []
    for rows_a, rows_b, pick in (
        (stage_a, stage_b, [0]),
        (near_a, near_b, [1, 3]),
        (final_a[2], final_b[2], [2]),
    ):
        cot_a = jnp.concatenate([grad_a[k] for k in pick], axis=0)
        cot_b = jnp.concatenate([grad_b[k] for k in pick], axis=0)
        parts_a.append(chunk_pass(rows_a, gate_weight[0], up_weight[0], cot_a))
        parts_b.append(chunk_pass(rows_b, gate_weight[1], up_weight[1], cot_b))

    def assemble(parts, lead, nxt):
        own, near, far = (p[0] for p in parts)
        plus, minus = near[:block], near[block:]
        rows = jnp.concatenate([own, plus, far, minus], axis=0)
        grads = [sum(p[i] for p in parts) for i in (1, 2)]
        return rows.reshape(lead, nxt, nz, owners, CAP, width), grads

    hid_a, (g_a, u_a) = assemble(parts_a, ny, nx)
    hid_b, (g_b, u_b) = assemble(parts_b, nx, ny)
    hidden = jnp.stack(
        [jnp.transpose(hid_a, (3, 0, 2, 1, 4, 5)), jnp.transpose(hid_b, (3, 1, 2, 0, 4, 5))], axis=0
    )
    hidden = jnp.roll(hidden, py, axis=2)
    hidden = jnp.roll(hidden, pz, axis=3)
    hidden = jnp.roll(hidden, px, axis=4)
    hidden = hidden.reshape(hidden_grad.shape)
    gate_grad = jnp.stack([g_a, g_b], axis=0)
    up_grad = jnp.stack([u_a, u_b], axis=0)
    return (hidden, gate_grad, up_grad)


def solution(mesh):
    grid = Mesh(mesh.devices.reshape(mesh.shape["expert"], 4, 2, -1), ("expert",) + FSDP_AXES)
    rows_spec = P(("expert",) + FSDP_AXES, None)
    expert_spec = P("expert", None, FSDP_AXES)
    in_specs = (rows_spec, rows_spec, expert_spec, expert_spec, expert_spec)
    out_specs = (expert_spec, expert_spec, expert_spec)
    return jax.shard_map(
        on_device, mesh=grid, in_specs=in_specs, out_specs=out_specs, check_vma=False
    )
```

```python
import jax
import jax.numpy as jnp
from jax import lax
from jax.sharding import Mesh
from jax.sharding import PartitionSpec as P

CAP = 24
FSDP_AXES = ("y", "zh", "x")


def shift(value, axis, step):
    size = lax.axis_size(axis)
    return lax.ppermute(value, axis, [(j, (j + step) % size) for j in range(size)])


def paired_ring(first, first_axis, second, second_axis):
    first_minus = shift(first, first_axis, 1)
    first_plus = shift(first, first_axis, -1)
    second_minus = shift(second, second_axis, 1)
    second_plus = shift(second, second_axis, -1)
    first_minus, first_plus = lax.optimization_barrier((first_minus, first_plus))
    second_minus, second_plus = lax.optimization_barrier((second_minus, second_plus))
    half = first.shape[0] // 2

    def far(minus, plus, axis):
        return shift(minus[:half], axis, 1), shift(plus[half:], axis, -1)

    first_lo, first_hi = far(first_minus, first_plus, first_axis)
    second_lo, second_hi = far(second_minus, second_plus, second_axis)
    first_lo, first_hi, second_lo, second_hi = lax.optimization_barrier(
        (first_lo, first_hi, second_lo, second_hi)
    )
    first_far = jnp.concatenate([first_lo, first_hi], axis=0)
    second_far = jnp.concatenate([second_lo, second_hi], axis=0)
    return [first, first_plus, first_far, first_minus], [second, second_plus, second_far, second_minus]


def chunk_pass(rows, gate_w, up_w, cotan):
    gate = jnp.dot(rows, gate_w, preferred_element_type=jnp.float32)
    upval = jnp.dot(rows, up_w, preferred_element_type=jnp.float32)
    cotan = cotan.astype(jnp.float32)
    sigma = 1.0 / (1.0 + jnp.exp(-gate))
    active = gate * sigma
    hidden = (active * upval).astype(jnp.bfloat16)
    gate_delta = (cotan * upval * sigma * (1.0 + gate * (1.0 - sigma))).astype(jnp.bfloat16)
    up_delta = (cotan * active).astype(jnp.bfloat16)
    gate_sum = jnp.dot(rows.T, gate_delta, preferred_element_type=jnp.float32)
    up_sum = jnp.dot(rows.T, up_delta, preferred_element_type=jnp.float32)
    return hidden, gate_sum, up_sum


def on_device(tokens, expert_ids, gate_weight, up_weight, hidden_grad):
    owners = lax.axis_size("expert")
    per_owner = gate_weight.shape[0]
    model = gate_weight.shape[1]
    width = gate_weight.shape[2]
    route = expert_ids[:, 0]
    total_experts = per_owner * owners
    onehot = (route[:, None] == jnp.arange(total_experts, dtype=jnp.int32)[None, :]).astype(
        jnp.int32
    )
    rank = jnp.sum((jnp.cumsum(onehot, axis=0) - onehot) * onehot, axis=1)
    owner_of = route // per_owner
    within = route % per_owner
    target = owner_of * (per_owner * CAP) + within * CAP + rank
    send_rows = per_owner * owners * CAP
    placing = (jnp.arange(send_rows, dtype=jnp.int32)[:, None] == target[None, :]).astype(
        jnp.bfloat16
    )
    outgoing = jnp.dot(placing, tokens, preferred_element_type=jnp.float32).astype(jnp.bfloat16)
    outgoing = outgoing.reshape(owners, per_owner, CAP, model)
    arrived = lax.all_to_all(outgoing, "expert", split_axis=0, concat_axis=0, tiled=True)
    by_expert = jnp.transpose(arrived, (1, 0, 2, 3)).reshape(per_owner, owners * CAP, model)

    ny, nz, nx = (lax.axis_size(a) for a in FSDP_AXES)
    py, pz, px = (lax.axis_index(a) for a in FSDP_AXES)
    local = [
        jnp.concatenate([by_expert[g], shift(by_expert[g], "zh", 1)], axis=0) for g in range(per_owner)
    ]
    stage_a, stage_b = paired_ring(local[0], "x", local[1], "y")
    stage_a = jnp.concatenate(stage_a, axis=0)
    stage_b = jnp.concatenate(stage_b, axis=0)
    final_a, final_b = paired_ring(stage_a, "y", stage_b, "x")
    near_a = jnp.concatenate([final_a[1], final_a[3]], axis=0)
    near_b = jnp.concatenate([final_b[1], final_b[3]], axis=0)

    grad = hidden_grad.reshape(per_owner, owners, ny, nz, nx, CAP, width)
    grad = jnp.roll(grad, -py, axis=2)
    grad = jnp.roll(grad, -pz, axis=3)
    grad = jnp.roll(grad, -px, axis=4)
    block = nx * nz * owners * CAP
    grad_a = jnp.transpose(grad[0], (1, 3, 2, 0, 4, 5)).reshape(ny, block, width)
    grad_b = jnp.transpose(grad[1], (3, 1, 2, 0, 4, 5)).reshape(nx, block, width)

    parts_a = []
    parts_b = []
    for rows_a, rows_b, pick in (
        (stage_a, stage_b, [0]),
        (near_a, near_b, [1, 3]),
        (final_a[2], final_b[2], [2]),
    ):
        cot_a = jnp.concatenate([grad_a[k] for k in pick], axis=0)
        cot_b = jnp.concatenate([grad_b[k] for k in pick], axis=0)
        parts_a.append(chunk_pass(rows_a, gate_weight[0], up_weight[0], cot_a))
        parts_b.append(chunk_pass(rows_b, gate_weight[1], up_weight[1], cot_b))

    def assemble(parts, lead, nxt):
        own, near, far = (p[0] for p in parts)
        plus, minus = near[:block], near[block:]
        rows = jnp.concatenate([own, plus, far, minus], axis=0)
        grads = [sum(p[i] for p in parts) for i in (1, 2)]
        return rows.reshape(lead, nxt, nz, owners, CAP, width), grads

    hid_a, (g_a, u_a) = assemble(parts_a, ny, nx)
    hid_b, (g_b, u_b) = assemble(parts_b, nx, ny)
    hidden = jnp.stack(
        [jnp.transpose(hid_a, (3, 0, 2, 1, 4, 5)), jnp.transpose(hid_b, (3, 1, 2, 0, 4, 5))], axis=0
    )
    hidden = jnp.roll(hidden, py, axis=2)
    hidden = jnp.roll(hidden, pz, axis=3)
    hidden = jnp.roll(hidden, px, axis=4)
    hidden = hidden.reshape(hidden_grad.shape)
    gate_grad = jnp.stack([g_a, g_b], axis=0)
    up_grad = jnp.stack([u_a, u_b], axis=0)
    return (hidden, gate_grad, up_grad)


def solution(mesh):
    grid = Mesh(mesh.devices.reshape(mesh.shape["expert"], 4, 2, -1), ("expert",) + FSDP_AXES)
    rows_spec = P(("expert",) + FSDP_AXES, None)
    expert_spec = P("expert", None, FSDP_AXES)
    in_specs = (rows_spec, rows_spec, expert_spec, expert_spec, expert_spec)
    out_specs = (expert_spec, expert_spec, expert_spec)
    return jax.shard_map(
        on_device, mesh=grid, in_specs=in_specs, out_specs=out_specs, check_vma=False
    )
```

```python
import jax
import jax.numpy as jnp
from jax import lax
from jax.sharding import Mesh
from jax.sharding import PartitionSpec as P

CAP = 24
FSDP_AXES = ("y", "zh", "x")


def shift(value, axis, step):
    size = lax.axis_size(axis)
    return lax.ppermute(value, axis, [(j, (j + step) % size) for j in range(size)])


def paired_ring(first, first_axis, second, second_axis, joint=True):
    first_minus = shift(first, first_axis, 1)
    first_plus = shift(first, first_axis, -1)
    second_minus = shift(second, second_axis, 1)
    second_plus = shift(second, second_axis, -1)
    if joint:
        first_minus, first_plus, second_minus, second_plus = lax.optimization_barrier(
            (first_minus, first_plus, second_minus, second_plus)
        )
    else:
        first_minus, first_plus = lax.optimization_barrier((first_minus, first_plus))
        second_minus, second_plus = lax.optimization_barrier((second_minus, second_plus))
    half = first.shape[0] // 2

    def far(minus, plus, axis):
        return shift(minus[:half], axis, 1), shift(plus[half:], axis, -1)

    first_lo, first_hi = far(first_minus, first_plus, first_axis)
    second_lo, second_hi = far(second_minus, second_plus, second_axis)
    first_lo, first_hi, second_lo, second_hi = lax.optimization_barrier(
        (first_lo, first_hi, second_lo, second_hi)
    )
    first_far = jnp.concatenate([first_lo, first_hi], axis=0)
    second_far = jnp.concatenate([second_lo, second_hi], axis=0)
    return [first, first_plus, first_far, first_minus], [second, second_plus, second_far, second_minus]


def chunk_pass(rows, gate_w, up_w, cotan):
    gate = jnp.dot(rows, gate_w, preferred_element_type=jnp.float32)
    upval = jnp.dot(rows, up_w, preferred_element_type=jnp.float32)
    cotan = cotan.astype(jnp.float32)
    sigma = 1.0 / (1.0 + jnp.exp(-gate))
    active = gate * sigma
    hidden = (active * upval).astype(jnp.bfloat16)
    gate_delta = (cotan * upval * sigma * (1.0 + gate * (1.0 - sigma))).astype(jnp.bfloat16)
    up_delta = (cotan * active).astype(jnp.bfloat16)
    gate_sum = jnp.dot(rows.T, gate_delta, preferred_element_type=jnp.float32)
    up_sum = jnp.dot(rows.T, up_delta, preferred_element_type=jnp.float32)
    return hidden, gate_sum, up_sum


def on_device(tokens, expert_ids, gate_weight, up_weight, hidden_grad):
    owners = lax.axis_size("expert")
    per_owner = gate_weight.shape[0]
    model = gate_weight.shape[1]
    width = gate_weight.shape[2]
    route = expert_ids[:, 0]
    total_experts = per_owner * owners
    onehot = (route[:, None] == jnp.arange(total_experts, dtype=jnp.int32)[None, :]).astype(
        jnp.int32
    )
    rank = jnp.sum((jnp.cumsum(onehot, axis=0) - onehot) * onehot, axis=1)
    owner_of = route // per_owner
    within = route % per_owner
    target = owner_of * (per_owner * CAP) + within * CAP + rank
    send_rows = per_owner * owners * CAP
    placing = (jnp.arange(send_rows, dtype=jnp.int32)[:, None] == target[None, :]).astype(
        jnp.bfloat16
    )
    outgoing = jnp.dot(placing, tokens, preferred_element_type=jnp.float32).astype(jnp.bfloat16)
    outgoing = outgoing.reshape(owners, per_owner, CAP, model)
    arrived = lax.all_to_all(outgoing, "expert", split_axis=0, concat_axis=0, tiled=True)
    by_expert = jnp.transpose(arrived, (1, 0, 2, 3)).reshape(per_owner, owners * CAP, model)

    ny, nz, nx = (lax.axis_size(a) for a in FSDP_AXES)
    py, pz, px = (lax.axis_index(a) for a in FSDP_AXES)
    local = [
        jnp.concatenate([by_expert[g], shift(by_expert[g], "zh", 1)], axis=0) for g in range(per_owner)
    ]
    stage_a, stage_b = paired_ring(local[0], "x", local[1], "y", joint=False)
    stage_a = jnp.concatenate(stage_a, axis=0)
    stage_b = jnp.concatenate(stage_b, axis=0)
    final_a, final_b = paired_ring(stage_a, "y", stage_b, "x")
    near_a = jnp.concatenate([final_a[1], final_a[3]], axis=0)
    near_b = jnp.concatenate([final_b[1], final_b[3]], axis=0)

    grad = hidden_grad.reshape(per_owner, owners, ny, nz, nx, CAP, width)
    grad = jnp.roll(grad, -py, axis=2)
    grad = jnp.roll(grad, -pz, axis=3)
    grad = jnp.roll(grad, -px, axis=4)
    block = nx * nz * owners * CAP
    grad_a = jnp.transpose(grad[0], (1, 3, 2, 0, 4, 5)).reshape(ny, block, width)
    grad_b = jnp.transpose(grad[1], (3, 1, 2, 0, 4, 5)).reshape(nx, block, width)

    parts_a = []
    parts_b = []
    for rows_a, rows_b, pick in (
        (stage_a, stage_b, [0]),
        (near_a, near_b, [1, 3]),
        (final_a[2], final_b[2], [2]),
    ):
        cot_a = jnp.concatenate([grad_a[k] for k in pick], axis=0)
        cot_b = jnp.concatenate([grad_b[k] for k in pick], axis=0)
        parts_a.append(chunk_pass(rows_a, gate_weight[0], up_weight[0], cot_a))
        parts_b.append(chunk_pass(rows_b, gate_weight[1], up_weight[1], cot_b))

    def assemble(parts, lead, nxt):
        own, near, far = (p[0] for p in parts)
        plus, minus = near[:block], near[block:]
        rows = jnp.concatenate([own, plus, far, minus], axis=0)
        grads = [sum(p[i] for p in parts) for i in (1, 2)]
        return rows.reshape(lead, nxt, nz, owners, CAP, width), grads

    hid_a, (g_a, u_a) = assemble(parts_a, ny, nx)
    hid_b, (g_b, u_b) = assemble(parts_b, nx, ny)
    hidden = jnp.stack(
        [jnp.transpose(hid_a, (3, 0, 2, 1, 4, 5)), jnp.transpose(hid_b, (3, 1, 2, 0, 4, 5))], axis=0
    )
    hidden = jnp.roll(hidden, py, axis=2)
    hidden = jnp.roll(hidden, pz, axis=3)
    hidden = jnp.roll(hidden, px, axis=4)
    hidden = hidden.reshape(hidden_grad.shape)
    gate_grad = jnp.stack([g_a, g_b], axis=0)
    up_grad = jnp.stack([u_a, u_b], axis=0)
    return (hidden, gate_grad, up_grad)


def solution(mesh):
    grid = Mesh(mesh.devices.reshape(mesh.shape["expert"], 4, 2, -1), ("expert",) + FSDP_AXES)
    rows_spec = P(("expert",) + FSDP_AXES, None)
    expert_spec = P("expert", None, FSDP_AXES)
    in_specs = (rows_spec, rows_spec, expert_spec, expert_spec, expert_spec)
    out_specs = (expert_spec, expert_spec, expert_spec)
    return jax.shard_map(
        on_device, mesh=grid, in_specs=in_specs, out_specs=out_specs, check_vma=False
    )
```

```python
import jax
import jax.numpy as jnp
from jax import lax
from jax.sharding import Mesh
from jax.sharding import PartitionSpec as P

CAP = 24
FSDP_AXES = ("y", "zh", "x")


def shift(value, axis, step):
    size = lax.axis_size(axis)
    return lax.ppermute(value, axis, [(j, (j + step) % size) for j in range(size)])


def paired_ring(first, first_axis, second, second_axis, joint=True):
    first_minus = shift(first, first_axis, 1)
    first_plus = shift(first, first_axis, -1)
    second_minus = shift(second, second_axis, 1)
    second_plus = shift(second, second_axis, -1)
    if joint:
        first_minus, first_plus, second_minus, second_plus = lax.optimization_barrier(
            (first_minus, first_plus, second_minus, second_plus)
        )
    else:
        first_minus, first_plus = lax.optimization_barrier((first_minus, first_plus))
        second_minus, second_plus = lax.optimization_barrier((second_minus, second_plus))
    half = first.shape[0] // 2

    def far(minus, plus, axis):
        return shift(minus[:half], axis, 1), shift(plus[half:], axis, -1)

    first_lo, first_hi = far(first_minus, first_plus, first_axis)
    second_lo, second_hi = far(second_minus, second_plus, second_axis)
    if joint:
        first_lo, first_hi, second_lo, second_hi = lax.optimization_barrier(
            (first_lo, first_hi, second_lo, second_hi)
        )
    else:
        first_lo, first_hi = lax.optimization_barrier((first_lo, first_hi))
        second_lo, second_hi = lax.optimization_barrier((second_lo, second_hi))
    first_far = jnp.concatenate([first_lo, first_hi], axis=0)
    second_far = jnp.concatenate([second_lo, second_hi], axis=0)
    return [first, first_plus, first_far, first_minus], [second, second_plus, second_far, second_minus]


def chunk_pass(rows, gate_w, up_w, cotan):
    gate = jnp.dot(rows, gate_w, preferred_element_type=jnp.float32)
    upval = jnp.dot(rows, up_w, preferred_element_type=jnp.float32)
    cotan = cotan.astype(jnp.float32)
    sigma = 1.0 / (1.0 + jnp.exp(-gate))
    active = gate * sigma
    hidden = (active * upval).astype(jnp.bfloat16)
    gate_delta = (cotan * upval * sigma * (1.0 + gate * (1.0 - sigma))).astype(jnp.bfloat16)
    up_delta = (cotan * active).astype(jnp.bfloat16)
    gate_sum = jnp.dot(rows.T, gate_delta, preferred_element_type=jnp.float32)
    up_sum = jnp.dot(rows.T, up_delta, preferred_element_type=jnp.float32)
    return hidden, gate_sum, up_sum


def on_device(tokens, expert_ids, gate_weight, up_weight, hidden_grad):
    owners = lax.axis_size("expert")
    per_owner = gate_weight.shape[0]
    model = gate_weight.shape[1]
    width = gate_weight.shape[2]
    route = expert_ids[:, 0]
    total_experts = per_owner * owners
    onehot = (route[:, None] == jnp.arange(total_experts, dtype=jnp.int32)[None, :]).astype(
        jnp.int32
    )
    rank = jnp.sum((jnp.cumsum(onehot, axis=0) - onehot) * onehot, axis=1)
    owner_of = route // per_owner
    within = route % per_owner
    target = owner_of * (per_owner * CAP) + within * CAP + rank
    send_rows = per_owner * owners * CAP
    placing = (jnp.arange(send_rows, dtype=jnp.int32)[:, None] == target[None, :]).astype(
        jnp.bfloat16
    )
    outgoing = jnp.dot(placing, tokens, preferred_element_type=jnp.float32).astype(jnp.bfloat16)
    outgoing = outgoing.reshape(owners, per_owner, CAP, model)
    arrived = lax.all_to_all(outgoing, "expert", split_axis=0, concat_axis=0, tiled=True)
    by_expert = jnp.transpose(arrived, (1, 0, 2, 3)).reshape(per_owner, owners * CAP, model)

    ny, nz, nx = (lax.axis_size(a) for a in FSDP_AXES)
    py, pz, px = (lax.axis_index(a) for a in FSDP_AXES)
    local = [
        jnp.concatenate([by_expert[g], shift(by_expert[g], "zh", 1)], axis=0) for g in range(per_owner)
    ]
    stage_a, stage_b = paired_ring(local[0], "x", local[1], "y", joint=False)
    stage_a = jnp.concatenate(stage_a, axis=0)
    stage_b = jnp.concatenate(stage_b, axis=0)
    final_a, final_b = paired_ring(stage_a, "y", stage_b, "x")
    near_a = jnp.concatenate([final_a[1], final_a[3]], axis=0)
    near_b = jnp.concatenate([final_b[1], final_b[3]], axis=0)

    grad = hidden_grad.reshape(per_owner, owners, ny, nz, nx, CAP, width)
    grad = jnp.roll(grad, -py, axis=2)
    grad = jnp.roll(grad, -pz, axis=3)
    grad = jnp.roll(grad, -px, axis=4)
    block = nx * nz * owners * CAP
    grad_a = jnp.transpose(grad[0], (1, 3, 2, 0, 4, 5)).reshape(ny, block, width)
    grad_b = jnp.transpose(grad[1], (3, 1, 2, 0, 4, 5)).reshape(nx, block, width)

    parts_a = []
    parts_b = []
    for rows_a, rows_b, pick in (
        (stage_a, stage_b, [0]),
        (near_a, near_b, [1, 3]),
        (final_a[2], final_b[2], [2]),
    ):
        cot_a = jnp.concatenate([grad_a[k] for k in pick], axis=0)
        cot_b = jnp.concatenate([grad_b[k] for k in pick], axis=0)
        parts_a.append(chunk_pass(rows_a, gate_weight[0], up_weight[0], cot_a))
        parts_b.append(chunk_pass(rows_b, gate_weight[1], up_weight[1], cot_b))

    def assemble(parts, lead, nxt):
        own, near, far = (p[0] for p in parts)
        plus, minus = near[:block], near[block:]
        rows = jnp.concatenate([own, plus, far, minus], axis=0)
        grads = [sum(p[i] for p in parts) for i in (1, 2)]
        return rows.reshape(lead, nxt, nz, owners, CAP, width), grads

    hid_a, (g_a, u_a) = assemble(parts_a, ny, nx)
    hid_b, (g_b, u_b) = assemble(parts_b, nx, ny)
    hidden = jnp.stack(
        [jnp.transpose(hid_a, (3, 0, 2, 1, 4, 5)), jnp.transpose(hid_b, (3, 1, 2, 0, 4, 5))], axis=0
    )
    hidden = jnp.roll(hidden, py, axis=2)
    hidden = jnp.roll(hidden, pz, axis=3)
    hidden = jnp.roll(hidden, px, axis=4)
    hidden = hidden.reshape(hidden_grad.shape)
    gate_grad = jnp.stack([g_a, g_b], axis=0)
    up_grad = jnp.stack([u_a, u_b], axis=0)
    return (hidden, gate_grad, up_grad)


def solution(mesh):
    grid = Mesh(mesh.devices.reshape(mesh.shape["expert"], 4, 2, -1), ("expert",) + FSDP_AXES)
    rows_spec = P(("expert",) + FSDP_AXES, None)
    expert_spec = P("expert", None, FSDP_AXES)
    in_specs = (rows_spec, rows_spec, expert_spec, expert_spec, expert_spec)
    out_specs = (expert_spec, expert_spec, expert_spec)
    return jax.shard_map(
        on_device, mesh=grid, in_specs=in_specs, out_specs=out_specs, check_vma=False
    )
```
